128 devices in a mesh: gx: 4 (over x), gy: 32 (over z, y, core).
Axes of the slice: x: 4, y: 4, z: 4, core: 2. Of those that a mesh axis runs over, the one named last changes fastest.
Arguments:
- src_points: bfloat16 [128, 1024, 128], P('gx'), may hold values from -0.47729708 to 0.47729708
- tgt_points: bfloat16 [128, 1024, 128], P(('gx', 'gy')), may hold values from -0.47729708 to 0.47729708
- src_log_mass: float32 [128, 1024], P('gx'), may hold values from -1 to 1
- tgt_log_mass: float32 [128, 1024], P(('gx', 'gy')), may hold values from -1 to 1
- near_pairs: int32 [768, 2], P(('gx', 'gy')), may hold values from 0 to 127, as said below
- target_slot: int32 [128], replicated, may hold values from 0 to 127, as said below
Outputs:
- f_pot: float32 [128, 1024], P('gx')
- g_pot: float32 [128, 1024], P(('gx', 'gy'))
- grad: float32 [128, 1024, 128], P(('gx', 'gy'))
The draws below stay inside these ranges and needn't reach their ends.
Inputs may be any that keep to these rules, and one draw needn't show every extreme that they name: `near_pairs`: row p belongs to the block p // 6 = a 32 + b. Its source cluster s satisfies s // 32 = a and (s % 32) // 1 lies in b - 2 to b + 2; the slot of its target cluster, target_slot of it, is held by a device of gy index b and gx index a - 1, a or a + 1 (slot = gx index 32 + gy index). No pair stands twice. Every source cluster and every target cluster is in some pair. `target_slot`: A permutation; each target cluster's slot has the same value of // 32 as the cluster's number.
All inputs are finite; a program needn't handle non-finite values.
Results may differ from the reference program's by a relative error of at most 0.00099.
Values may be sent and summed in bfloat16 or wider, within the bound.
No kernel may reach another device: no remote copies, remote signals or barrier semaphores. Data moves between devices by JAX's collectives and lax.ppermute only.
A program may use at most 64 MiB of HBM per device.

```python
import math
import jax
import jax.numpy as jnp
from jax import lax

D = 128
CS = 1024
ITERS = 3
CL_DEV = 1
PAIR_DEV = 6
NS = 128
NT = 128
N_GX = 4
N_GY = 32


def point_cloud(key, count):
    key_centre, key_noise = jax.random.split(key)
    spread = 1.0 / math.sqrt(D)
    centre = jnp.clip(0.35 * jax.random.normal(key_centre, (count, 1, D), jnp.float32), -1.4, 1.4)
    noise = jnp.clip(jax.random.normal(key_noise, (count, CS, D), jnp.float32), -4.0, 4.0)
    return ((centre + noise) * spread).astype(jnp.bfloat16)


def draw_src_points(key, part):
    return point_cloud(jax.random.fold_in(key, 21), CL_DEV * N_GX * N_GY)


def draw_tgt_points(key, part):
    return point_cloud(jax.random.fold_in(key, 22), CL_DEV * N_GX * N_GY)


def pair_plan(key):
    group = N_GY * CL_DEV
    devices = N_GX * N_GY
    width_tgt = 3 * CL_DEV
    width_src = 5 * CL_DEV
    key_slot, key_choose = jax.random.split(jax.random.fold_in(key, 31), 2)
    base_ids = jnp.arange(group, dtype=jnp.int32)
    slot_keys = jax.random.randint(key_slot, (N_GX, group), 0, 1 << 20, jnp.int32) * 64 + base_ids[None, :]
    id_of_slot = jnp.argsort(slot_keys, axis=1).astype(jnp.int32)
    device_ids = jnp.arange(devices, dtype=jnp.int32)
    gx_of = device_ids // N_GY
    gy_of = device_ids % N_GY
    candidate = jnp.arange(width_src * width_tgt, dtype=jnp.int32)
    cand_src_rel = candidate // width_tgt
    cand_window = candidate % width_tgt
    cand_offset = cand_window // CL_DEV
    cand_local = cand_window % CL_DEV
    owner_gx = gx_of[:, None] - 1 + cand_offset[None, :]
    src_local = (gy_of[:, None] - 2) * CL_DEV + cand_src_rel[None, :]
    inside = (owner_gx >= 0) & (owner_gx < N_GX) & (src_local >= 0) & (src_local < group)
    is_forced = (cand_offset[None, :] == 1) & (cand_src_rel[None, :] == 2 * CL_DEV + cand_local[None, :])
    scores = jax.random.randint(key_choose, (devices, width_src * width_tgt), 0, 1 << 18, jnp.int32) * 4096 + candidate[None, :]
    scores = jnp.where(inside & jnp.logical_not(is_forced), scores, -1)
    chosen = lax.top_k(scores, PAIR_DEV - CL_DEV)[1]
    own_local = jnp.arange(CL_DEV, dtype=jnp.int32)
    fixed_source = gy_of[:, None] * CL_DEV + own_local[None, :]
    fixed_window = jnp.broadcast_to(CL_DEV + own_local[None, :], (devices, CL_DEV))
    chosen_source = jnp.take_along_axis(src_local, chosen, axis=1)
    all_source = jnp.concatenate([fixed_source, chosen_source], axis=1)
    all_window = jnp.concatenate([fixed_window, cand_window[chosen]], axis=1)
    slot_ids = ((gx_of[:, None] - 1 + all_window // CL_DEV) * N_GY + gy_of[:, None]) * CL_DEV + all_window % CL_DEV
    target_ids = slot_ids // group * group + id_of_slot[slot_ids // group, slot_ids % group]
    source_ids = gx_of[:, None] * group + all_source
    near_pairs = jnp.stack([source_ids, target_ids], axis=-1).reshape(devices * PAIR_DEV, 2).astype(jnp.int32)
    slot_of_id = jnp.argsort(id_of_slot, axis=1).astype(jnp.int32)
    target_slot = (jnp.arange(N_GX, dtype=jnp.int32)[:, None] * group + slot_of_id).reshape(-1)
    return (near_pairs, target_slot)


def draw_near_pairs(key, part):
    return pair_plan(key)[0]


def draw_target_slot(key, part):
    return pair_plan(key)[1]


def block_levels(key, extent, pieces, smallest, top_value):
    def one(dim, parts):
        draws = jax.random.uniform(jax.random.fold_in(jax.random.fold_in(key, 6), dim), (parts,), jnp.float32, smallest / len(pieces), top_value / len(pieces))
        return jnp.repeat(jnp.exp(draws), extent[dim] // parts).reshape((-1,) + (1,) * (len(extent) - dim - 1))

    level = one(*pieces[0])
    for cut in pieces[1:]:
        level = level * one(*cut)
    return level


def setup_inputs(seed: int = 0) -> dict:
    arg_keys = jax.random.split(jax.random.key(seed), 7)
    src_points = draw_src_points(jax.random.fold_in(arg_keys[6], 71), 0)
    tgt_points = draw_tgt_points(jax.random.fold_in(arg_keys[6], 71), 0)
    src_log_mass = jnp.clip(jax.random.uniform(arg_keys[2], (NS, CS), jnp.float32, -1.0, 1.0) * block_levels(arg_keys[2], (NS, CS), ((0, 4),), -0.4, 0.0), -1.0, 1.0)
    tgt_log_mass = jnp.clip(jax.random.uniform(arg_keys[3], (NT, CS), jnp.float32, -1.0, 1.0) * block_levels(arg_keys[3], (NT, CS), ((0, 128),), -0.4, 0.0), -1.0, 1.0)
    near_pairs = draw_near_pairs(jax.random.fold_in(arg_keys[6], 71), 0)
    target_slot = draw_target_slot(jax.random.fold_in(arg_keys[6], 71), 0)
    return dict(src_points=src_points, tgt_points=tgt_points, src_log_mass=src_log_mass, tgt_log_mass=tgt_log_mass, near_pairs=near_pairs, target_slot=target_slot)


EPSILON = 0.03
EMPTY_LOG = -1e+30

def log_add(first, second):
    peak_val = jnp.maximum(first, second)
    return peak_val + jnp.log(jnp.exp(first - peak_val) + jnp.exp(second - peak_val))

def cost_tile(src_rows, tgt_rows):
    src_sq = lax.optimization_barrier(jnp.sum(jnp.square(src_rows.astype(jnp.float32)), axis=1))
    tgt_sq = lax.optimization_barrier(jnp.sum(jnp.square(tgt_rows.astype(jnp.float32)), axis=1))
    inner = jnp.dot(src_rows, tgt_rows.T, preferred_element_type=jnp.float32)
    return 0.5 * (src_sq[:, None] + tgt_sq[None, :]) - inner

def pick(table, position):
    return lax.dynamic_index_in_dim(table, position, 0, keepdims=False)

def reference(src_points, tgt_points, src_log_mass, tgt_log_mass, near_pairs, target_slot):
    num_src = src_points.shape[0]
    num_tgt = tgt_points.shape[0]
    source_ids = near_pairs[:, 0].astype(jnp.int32)
    slot_ids = target_slot[near_pairs[:, 1]].astype(jnp.int32)
    pair_order = jnp.arange(near_pairs.shape[0], dtype=jnp.int32)
    g_pot = jnp.zeros((num_tgt, CS), jnp.float32)
    f_pot = jnp.zeros((num_src, CS), jnp.float32)
    for sweep_index in range(ITERS):

        def row_update(running, pair_index):
            source = source_ids[pair_index]
            target = slot_ids[pair_index]
            costs = cost_tile(pick(src_points, source), pick(tgt_points, target))
            scores = (pick(g_pot, target)[None, :] - costs) / EPSILON
            peak_val = lax.optimization_barrier(jnp.max(scores, axis=1))
            partial_value = peak_val + jnp.log(lax.optimization_barrier(jnp.sum(jnp.exp(scores - peak_val[:, None]), axis=1)))
            current = pick(running, source)
            return (lax.dynamic_update_index_in_dim(running, log_add(current, partial_value), source, 0), None)
        rows_total = lax.scan(row_update, jnp.full((num_src, CS), EMPTY_LOG, jnp.float32), pair_order)[0]
        f_pot = EPSILON * src_log_mass - EPSILON * rows_total

        def column_update(running, pair_index):
            source = source_ids[pair_index]
            target = slot_ids[pair_index]
            costs = cost_tile(pick(src_points, source), pick(tgt_points, target))
            scores = (pick(f_pot, source)[:, None] - costs) / EPSILON
            peak_val = lax.optimization_barrier(jnp.max(scores, axis=0))
            partial_value = peak_val + jnp.log(lax.optimization_barrier(jnp.sum(jnp.exp(scores - peak_val[None, :]), axis=0)))
            current = pick(running, target)
            return (lax.dynamic_update_index_in_dim(running, log_add(current, partial_value), target, 0), None)
        cols_total = lax.scan(column_update, jnp.full((num_tgt, CS), EMPTY_LOG, jnp.float32), pair_order)[0]
        g_pot = EPSILON * tgt_log_mass - EPSILON * cols_total
    group_size = num_src // N_GX

    def device_part(gx_pos, gy_pos):
        first = (gx_pos * N_GY + gy_pos) * PAIR_DEV

        def grad_update(totals, offset):
            pair_index = first + offset
            source = source_ids[pair_index]
            target = slot_ids[pair_index]
            local = source - gx_pos * group_size
            tgt_rows = pick(tgt_points, target)
            costs = cost_tile(pick(src_points, source), tgt_rows)
            weights = jnp.exp((pick(f_pot, source)[:, None] + pick(g_pot, target)[None, :] - costs) / EPSILON)
            mass_sum, moved = totals
            mass_sum = lax.dynamic_update_index_in_dim(mass_sum, pick(mass_sum, local) + lax.optimization_barrier(jnp.sum(weights, axis=1)), local, 0)
            product = jnp.dot(weights.astype(jnp.bfloat16), tgt_rows, preferred_element_type=jnp.float32)
            moved = lax.dynamic_update_index_in_dim(moved, pick(moved, local) + product, local, 0)
            return ((mass_sum, moved), None)
        start_vals = (jnp.zeros((group_size, CS), jnp.float32), jnp.zeros((group_size, CS, D), jnp.float32))
        mass_sum, moved = lax.scan(grad_update, start_vals, jnp.arange(PAIR_DEV, dtype=jnp.int32))[0]
        group_src = lax.dynamic_slice_in_dim(src_points, gx_pos * group_size, group_size, 0)
        return mass_sum[:, :, None] * group_src.astype(jnp.float32) - moved

    def group_grad(unused, gx_pos):

        def add_part(total, gy_pos):
            return (total + device_part(gx_pos, gy_pos), None)
        total = lax.scan(add_part, jnp.zeros((group_size, CS, D), jnp.float32), jnp.arange(N_GY, dtype=jnp.int32))[0]
        return (unused, total)
    grad = lax.scan(group_grad, jnp.zeros((), jnp.float32), jnp.arange(N_GX, dtype=jnp.int32))[1]
    return (f_pot, g_pot, grad.reshape(num_src, CS, D))
```

```python
import jax
import jax.numpy as jnp
from jax import lax
from jax.sharding import PartitionSpec as P

ITERS = 3


EPSILON = 0.03
EMPTY_LOG = -1e30


def padded(block, sides, width):
    for axis, dim in sides:
        count = lax.axis_size(axis)
        forward = [(i, i + 1) for i in range(count - 1)]
        backward = [(target, source) for source, target in forward]
        low = lax.ppermute(
            lax.slice_in_dim(block, block.shape[dim] - width, None, axis=dim), axis, forward
        )
        high = lax.ppermute(lax.slice_in_dim(block, 0, width, axis=dim), axis, backward)
        block = jnp.concatenate([low, block, high], axis=dim)
    return block


def passed_along(block, axis, distance):
    devices = range(lax.axis_size(axis))
    route = [(i - distance, i) for i in devices if i - distance in devices]
    return lax.ppermute(block, axis, route)


def log_add(first, second):
    peak_val = jnp.maximum(first, second)
    return peak_val + jnp.log(jnp.exp(first - peak_val) + jnp.exp(second - peak_val))


def pick(table, position):
    return lax.dynamic_index_in_dim(table, position, 0, keepdims=False)


def cost_tile(src_rows, tgt_rows, src_sq, tgt_sq):
    inner = lax.dot_general(
        src_rows, tgt_rows, (((1,), (1,)), ((), ())), preferred_element_type=jnp.float32
    )
    return 0.5 * (src_sq[:, None] + tgt_sq[None, :]) - inner


def squares(points):
    return jnp.sum(jnp.square(points.astype(jnp.float32)), axis=-1)


def fetch_points(tgt_points):
    window_pts = padded(tgt_points, (("gx", 0),), tgt_points.shape[0])
    return (window_pts, squares(window_pts))


def fetch_potential(g_local):
    return padded(g_local, (("gx", 0),), g_local.shape[0])


def body(src_points, tgt_points, src_log_mass, tgt_log_mass, near_pairs, target_slot):
    owned = tgt_points.shape[0]
    group_size = src_points.shape[0]
    cluster_pts = src_points.shape[1]
    coords = src_points.shape[2]
    gx_count = lax.axis_size("gx")
    gy_count = lax.axis_size("gy")
    gx_index = lax.axis_index("gx")
    gy_index = lax.axis_index("gy")
    source_local = near_pairs[:, 0] - gx_index * group_size
    matches = (
        near_pairs[:, 1][:, None] == jnp.arange(target_slot.shape[0], dtype=jnp.int32)[None, :]
    )
    slot_ids = jnp.sum(jnp.where(matches, target_slot[None, :], 0), axis=1)
    window_ids = (slot_ids // owned // gy_count - gx_index + 1) * owned + slot_ids % owned
    pair_order = jnp.arange(near_pairs.shape[0], dtype=jnp.int32)
    src_sq = squares(src_points)
    g_local = jnp.zeros((owned, cluster_pts), jnp.float32)
    g_window = jnp.zeros((3 * owned, cluster_pts), jnp.float32)
    span_ids = source_local - (gy_index - 2) * owned
    for sweep_index in range(ITERS):
        window_pts, window_sq = fetch_points(tgt_points)
        if sweep_index > 0:
            g_window = fetch_potential(g_local)

        def row_update(running, pair_index):
            source = source_local[pair_index]
            target = window_ids[pair_index]
            costs = cost_tile(
                pick(src_points, source),
                pick(window_pts, target),
                pick(src_sq, source),
                pick(window_sq, target),
            )
            scores = (pick(g_window, target)[None, :] - costs) / EPSILON
            peak_val = jnp.max(scores, axis=1)
            partial_value = peak_val + jnp.log(jnp.sum(jnp.exp(scores - peak_val[:, None]), axis=1))
            current = pick(running, source)
            return (
                lax.dynamic_update_index_in_dim(
                    running, log_add(current, partial_value), source, 0
                ),
                None,
            )

        rows_part = lax.scan(
            row_update, jnp.full((group_size, cluster_pts), EMPTY_LOG, jnp.float32), pair_order
        )[0]
        own_total = pick(rows_part, gy_index)
        for distance in (1, 2, -1, -2):
            sent = pick(rows_part, jnp.clip(gy_index + distance, 0, gy_count - 1))
            got = passed_along(sent, "gy", distance)
            has_sender = (gy_index - distance >= 0) & (gy_index - distance < gy_count)
            own_total = log_add(own_total, jnp.where(has_sender, got, EMPTY_LOG))
        f_own = EPSILON * pick(src_log_mass, gy_index) - EPSILON * own_total
        f_span = [passed_along(f_own, "gy", -d) for d in (-2, -1)]
        f_span = f_span + [f_own] + [passed_along(f_own, "gy", -d) for d in (1, 2)]
        f_span = jnp.stack(f_span)

        def column_update(running, pair_index):
            source = source_local[pair_index]
            target = window_ids[pair_index]
            costs = cost_tile(
                pick(src_points, source),
                pick(window_pts, target),
                pick(src_sq, source),
                pick(window_sq, target),
            )
            scores = (pick(f_span, span_ids[pair_index])[:, None] - costs) / EPSILON
            peak_val = jnp.max(scores, axis=0)
            partial_value = peak_val + jnp.log(jnp.sum(jnp.exp(scores - peak_val[None, :]), axis=0))
            current = pick(running, target)
            return (
                lax.dynamic_update_index_in_dim(
                    running, log_add(current, partial_value), target, 0
                ),
                None,
            )

        cols_part = lax.scan(
            column_update, jnp.full((3 * owned, cluster_pts), EMPTY_LOG, jnp.float32), pair_order
        )[0]
        from_left = passed_along(cols_part[2 * owned :], "gx", 1)
        from_right = passed_along(cols_part[:owned], "gx", -1)
        from_left = jnp.where(gx_index > 0, from_left, EMPTY_LOG)
        from_right = jnp.where(gx_index < gx_count - 1, from_right, EMPTY_LOG)
        cols_total = log_add(log_add(cols_part[owned : 2 * owned], from_left), from_right)
        g_local = EPSILON * tgt_log_mass - EPSILON * cols_total
    window_pts, window_sq = fetch_points(tgt_points)
    g_window = fetch_potential(g_local)
    span_rows = 5 * owned
    f_pot = lax.all_gather(f_own[None], "gy", axis=0, tiled=True)

    def grad_update(totals, pair_index):
        source = source_local[pair_index]
        row = span_ids[pair_index]
        target = window_ids[pair_index]
        tgt_rows = pick(window_pts, target)
        costs = cost_tile(
            pick(src_points, source), tgt_rows, pick(src_sq, source), pick(window_sq, target)
        )
        weights = jnp.exp(
            (pick(f_span, row)[:, None] + pick(g_window, target)[None, :] - costs) / EPSILON
        )
        mass_sum, moved = totals
        mass_sum = lax.dynamic_update_index_in_dim(
            mass_sum, pick(mass_sum, row) + jnp.sum(weights, axis=1), row, 0
        )
        product = jnp.dot(
            weights.astype(jnp.bfloat16), tgt_rows, preferred_element_type=jnp.float32
        )
        moved = lax.dynamic_update_index_in_dim(moved, pick(moved, row) + product, row, 0)
        return ((mass_sum, moved), None)

    start_vals = (
        jnp.zeros((span_rows, cluster_pts), jnp.float32),
        jnp.zeros((span_rows, cluster_pts, coords), jnp.float32),
    )
    mass_sum, moved = lax.scan(grad_update, start_vals, pair_order)[0]
    padding = jnp.zeros((2 * owned, cluster_pts, coords), src_points.dtype)
    padded_src = jnp.concatenate([padding, src_points, padding], axis=0)
    window_src = lax.dynamic_slice_in_dim(padded_src, gy_index * owned, span_rows, 0)
    span_parts = mass_sum[:, :, None] * window_src.astype(jnp.float32) - moved
    grad = span_parts[2 * owned : 3 * owned]
    for distance in (1, 2):
        upper = passed_along(
            span_parts[(2 - distance) * owned : (3 - distance) * owned], "gy", -distance
        )
        lower = passed_along(
            span_parts[(2 + distance) * owned : (3 + distance) * owned], "gy", distance
        )
        grad = grad + upper + lower
    return (f_pot, g_local, grad)


def solution(mesh):
    in_specs = (
        P("gx", None, None),
        P(("gx", "gy"), None, None),
        P("gx", None),
        P(("gx", "gy"), None),
        P(("gx", "gy"), None),
        P(),
    )
    out_specs = (P("gx", None), P(("gx", "gy"), None), P(("gx", "gy"), None, None))
    return jax.shard_map(body, mesh=mesh, in_specs=in_specs, out_specs=out_specs, check_vma=False)
```

```python
import jax
import jax.numpy as jnp
from jax import lax
from jax.sharding import PartitionSpec as P
from jax.experimental import pallas as pl
from jax.experimental.pallas import tpu as pltpu

ITERS = 3


EMPTY_LOG = -1e30


def padded(block, sides, width):
    for axis, dim in sides:
        count = lax.axis_size(axis)
        forward = [(i, i + 1) for i in range(count - 1)]
        backward = [(target, source) for source, target in forward]
        low = lax.ppermute(
            lax.slice_in_dim(block, block.shape[dim] - width, None, axis=dim), axis, forward
        )
        high = lax.ppermute(lax.slice_in_dim(block, 0, width, axis=dim), axis, backward)
        block = jnp.concatenate([low, block, high], axis=dim)
    return block


def passed_along(block, axis, distance):
    devices = range(lax.axis_size(axis))
    route = [(i - distance, i) for i in devices if i - distance in devices]
    return lax.ppermute(block, axis, route)


def log_add(first, second):
    peak_val = jnp.maximum(first, second)
    return peak_val + jnp.log(jnp.exp(first - peak_val) + jnp.exp(second - peak_val))


def pick(table, position):
    return lax.dynamic_index_in_dim(table, position, 0, keepdims=False)


def cost_tile(src_rows, tgt_rows, src_sq, tgt_sq):
    inner = lax.dot_general(
        src_rows, tgt_rows, (((1,), (1,)), ((), ())), preferred_element_type=jnp.float32
    )
    return 0.5 * (src_sq[:, None] + tgt_sq[None, :]) - inner


def squares(points):
    return jnp.sum(jnp.square(points.astype(jnp.float32)), axis=-1)


def fetch_points(tgt_points):
    window_pts = padded(tgt_points, (("gx", 0),), tgt_points.shape[0])
    return (window_pts, squares(window_pts))


def fetch_potential(g_local):
    return padded(g_local, (("gx", 0),), g_local.shape[0])


EPSILON = 0.03
INV_EPS = 1.0 / EPSILON
CHUNK = 256


def _lse_kernel(a_ids, b_ids, a_ref, b_ref, v_ref, o_ref):
    tile = lax.dot_general(
        b_ref[0], a_ref[0], (((1,), (1,)), ((), ())), preferred_element_type=jnp.float32
    )
    scores = tile * INV_EPS + v_ref[0]
    peak = jnp.max(scores, axis=0, keepdims=True)
    total = jnp.sum(jnp.exp(scores - peak), axis=0, keepdims=True)
    o_ref[0] = peak + jnp.log(total)


def pair_lse(a_ids, b_ids, a_pts, b_pts, v_col, interpret=False):
    pairs = a_ids.shape[0]
    rows = a_pts.shape[1]
    coords = a_pts.shape[2]
    cols = b_pts.shape[1]
    spec = pltpu.PrefetchScalarGridSpec(
        num_scalar_prefetch=2,
        grid=(pairs, rows // CHUNK),
        in_specs=[
            pl.BlockSpec((1, CHUNK, coords), lambda p, c, ai, bi: (ai[p], c, 0)),
            pl.BlockSpec((1, cols, coords), lambda p, c, ai, bi: (bi[p], 0, 0)),
            pl.BlockSpec((1, cols, 1), lambda p, c, ai, bi: (p, 0, 0)),
        ],
        out_specs=pl.BlockSpec((1, 1, CHUNK), lambda p, c, ai, bi: (p, 0, c)),
    )
    return pl.pallas_call(
        _lse_kernel,
        grid_spec=spec,
        out_shape=jax.ShapeDtypeStruct((pairs, 1, rows), jnp.float32),
        interpret=interpret,
    )(a_ids, b_ids, a_pts, b_pts, v_col)


def _grad_kernel(a_ids, b_ids, a_ref, b_ref, v_ref, w_ref, o_ref):
    src = a_ref[0]
    tgt = b_ref[0]
    tile = lax.dot_general(src, tgt, (((1,), (1,)), ((), ())), preferred_element_type=jnp.float32)
    weights = jnp.exp(tile * INV_EPS + v_ref[0] + w_ref[0])
    mass = jnp.sum(weights, axis=1, keepdims=True)
    moved = jnp.dot(weights.astype(jnp.bfloat16), tgt, preferred_element_type=jnp.float32)
    o_ref[0] = mass * src.astype(jnp.float32) - moved


def pair_grad(a_ids, b_ids, a_pts, b_pts, v_row, w_col, interpret=False):
    pairs = a_ids.shape[0]
    rows = a_pts.shape[1]
    coords = a_pts.shape[2]
    cols = b_pts.shape[1]
    spec = pltpu.PrefetchScalarGridSpec(
        num_scalar_prefetch=2,
        grid=(pairs, rows // CHUNK),
        in_specs=[
            pl.BlockSpec((1, CHUNK, coords), lambda p, c, ai, bi: (ai[p], c, 0)),
            pl.BlockSpec((1, cols, coords), lambda p, c, ai, bi: (bi[p], 0, 0)),
            pl.BlockSpec((1, 1, cols), lambda p, c, ai, bi: (p, 0, 0)),
            pl.BlockSpec((1, CHUNK, 1), lambda p, c, ai, bi: (p, c, 0)),
        ],
        out_specs=pl.BlockSpec((1, CHUNK, coords), lambda p, c, ai, bi: (p, c, 0)),
    )
    return pl.pallas_call(
        _grad_kernel,
        grid_spec=spec,
        out_shape=jax.ShapeDtypeStruct((pairs, rows, coords), jnp.float32),
        interpret=interpret,
    )(a_ids, b_ids, a_pts, b_pts, v_row, w_col)


def grouped_lse(mask, values):
    masked = jnp.where(mask[:, :, None], values[None], EMPTY_LOG)
    peak_val = jnp.max(masked, axis=1)
    return peak_val + jnp.log(jnp.sum(jnp.exp(masked - peak_val[:, None]), axis=1))


def body(src_points, tgt_points, src_log_mass, tgt_log_mass, near_pairs, target_slot):
    owned = tgt_points.shape[0]
    group_size = src_points.shape[0]
    gx_count = lax.axis_size("gx")
    gy_count = lax.axis_size("gy")
    gx_index = lax.axis_index("gx")
    gy_index = lax.axis_index("gy")
    source_local = jnp.clip(near_pairs[:, 0] - gx_index * group_size, 0, group_size - 1)
    matches = (
        near_pairs[:, 1][:, None] == jnp.arange(target_slot.shape[0], dtype=jnp.int32)[None, :]
    )
    slot_ids = jnp.sum(jnp.where(matches, target_slot[None, :], 0), axis=1)
    window_ids = (slot_ids // owned // gy_count - gx_index + 1) * owned + slot_ids % owned
    window_ids = jnp.clip(window_ids, 0, 3 * owned - 1)
    span_ids = jnp.clip(source_local - (gy_index - 2) * owned, 0, 5 * owned - 1)
    span_mask = span_ids[None, :] == jnp.arange(5 * owned, dtype=jnp.int32)[:, None]
    window_mask = window_ids[None, :] == jnp.arange(3 * owned, dtype=jnp.int32)[:, None]
    src_sq = squares(src_points)
    pair_src_sq = src_sq[source_local]
    window_pts, window_sq = fetch_points(tgt_points)
    pair_tgt_sq = window_sq[window_ids]
    g_local = None
    g_window = jnp.zeros((3 * owned, src_points.shape[1]), jnp.float32)
    for sweep_index in range(ITERS):
        if sweep_index > 0:
            g_window = fetch_potential(g_local)
        v_row = (g_window[window_ids] - 0.5 * pair_tgt_sq) / EPSILON
        part = pair_lse(source_local, window_ids, src_points, window_pts, v_row[:, :, None])
        part = part[:, 0] - 0.5 * pair_src_sq / EPSILON
        rows_span = grouped_lse(span_mask, part)
        own_total = rows_span[2]
        for distance in (1, 2, -1, -2):
            got = passed_along(rows_span[2 + distance], "gy", distance)
            has_sender = (gy_index - distance >= 0) & (gy_index - distance < gy_count)
            own_total = log_add(own_total, jnp.where(has_sender, got, EMPTY_LOG))
        f_own = EPSILON * pick(src_log_mass, gy_index) - EPSILON * own_total
        f_span = [passed_along(f_own, "gy", -d) for d in (-2, -1)]
        f_span = f_span + [f_own] + [passed_along(f_own, "gy", -d) for d in (1, 2)]
        f_span = jnp.stack(f_span)
        v_col = (f_span[span_ids] - 0.5 * pair_src_sq) / EPSILON
        part = pair_lse(window_ids, source_local, window_pts, src_points, v_col[:, :, None])
        part = part[:, 0] - 0.5 * pair_tgt_sq / EPSILON
        cols_part = grouped_lse(window_mask, part)
        from_left = passed_along(cols_part[2 * owned :], "gx", 1)
        from_right = passed_along(cols_part[:owned], "gx", -1)
        from_left = jnp.where(gx_index > 0, from_left, EMPTY_LOG)
        from_right = jnp.where(gx_index < gx_count - 1, from_right, EMPTY_LOG)
        cols_total = log_add(log_add(cols_part[owned : 2 * owned], from_left), from_right)
        g_local = EPSILON * tgt_log_mass - EPSILON * cols_total
    f_pot = lax.all_gather(f_own[None], "gy", axis=0, tiled=True)
    g_window = fetch_potential(g_local)
    v_row = (g_window[window_ids] - 0.5 * pair_tgt_sq) / EPSILON
    w_col = (f_span[span_ids] - 0.5 * pair_src_sq) / EPSILON
    contrib = pair_grad(
        source_local, window_ids, src_points, window_pts, v_row[:, None, :], w_col[:, :, None]
    )
    span_parts = jnp.sum(jnp.where(span_mask[:, :, None, None], contrib[None], 0.0), axis=1)
    grad = span_parts[2 * owned : 3 * owned]
    for distance in (1, 2):
        upper = passed_along(
            span_parts[(2 - distance) * owned : (3 - distance) * owned], "gy", -distance
        )
        lower = passed_along(
            span_parts[(2 + distance) * owned : (3 + distance) * owned], "gy", distance
        )
        grad = grad + upper + lower
    return (f_pot, g_local, grad)


def solution(mesh):
    in_specs = (
        P("gx", None, None),
        P(("gx", "gy"), None, None),
        P("gx", None),
        P(("gx", "gy"), None),
        P(("gx", "gy"), None),
        P(),
    )
    out_specs = (P("gx", None), P(("gx", "gy"), None), P(("gx", "gy"), None, None))
    return jax.shard_map(body, mesh=mesh, in_specs=in_specs, out_specs=out_specs, check_vma=False)
```

```python
import jax
import jax.numpy as jnp
from jax import lax
from jax.sharding import PartitionSpec as P
from jax.experimental import pallas as pl
from jax.experimental.pallas import tpu as pltpu

ITERS = 3


EMPTY_LOG = -1e30


def padded(block, sides, width):
    for axis, dim in sides:
        count = lax.axis_size(axis)
        forward = [(i, i + 1) for i in range(count - 1)]
        backward = [(target, source) for source, target in forward]
        low = lax.ppermute(
            lax.slice_in_dim(block, block.shape[dim] - width, None, axis=dim), axis, forward
        )
        high = lax.ppermute(lax.slice_in_dim(block, 0, width, axis=dim), axis, backward)
        block = jnp.concatenate([low, block, high], axis=dim)
    return block


def passed_along(block, axis, distance):
    devices = range(lax.axis_size(axis))
    route = [(i - distance, i) for i in devices if i - distance in devices]
    return lax.ppermute(block, axis, route)


def log_add(first, second):
    peak_val = jnp.maximum(first, second)
    return peak_val + jnp.log(jnp.exp(first - peak_val) + jnp.exp(second - peak_val))


def pick(table, position):
    return lax.dynamic_index_in_dim(table, position, 0, keepdims=False)


def cost_tile(src_rows, tgt_rows, src_sq, tgt_sq):
    inner = lax.dot_general(
        src_rows, tgt_rows, (((1,), (1,)), ((), ())), preferred_element_type=jnp.float32
    )
    return 0.5 * (src_sq[:, None] + tgt_sq[None, :]) - inner


def squares(points):
    return jnp.sum(jnp.square(points.astype(jnp.float32)), axis=-1)


def fetch_points(tgt_points):
    window_pts = padded(tgt_points, (("gx", 0),), tgt_points.shape[0])
    return (window_pts, squares(window_pts))


def fetch_potential(g_local):
    return padded(g_local, (("gx", 0),), g_local.shape[0])


EPSILON = 0.03
INV_EPS = 1.0 / EPSILON
CHUNK = 512


def _lse_kernel(a_ids, b_ids, a_ref, b_ref, v_ref, o_ref):
    tile = lax.dot_general(
        b_ref[0], a_ref[0], (((1,), (1,)), ((), ())), preferred_element_type=jnp.float32
    )
    scores = tile * INV_EPS + v_ref[0]
    peak = jnp.max(scores, axis=0, keepdims=True)
    total = jnp.sum(jnp.exp(scores - peak), axis=0, keepdims=True)
    o_ref[0] = peak + jnp.log(total)


def pair_lse(a_ids, b_ids, a_pts, b_pts, v_col, interpret=False):
    pairs = a_ids.shape[0]
    rows = a_pts.shape[1]
    coords = a_pts.shape[2]
    cols = b_pts.shape[1]
    spec = pltpu.PrefetchScalarGridSpec(
        num_scalar_prefetch=2,
        grid=(pairs, rows // CHUNK),
        in_specs=[
            pl.BlockSpec((1, CHUNK, coords), lambda p, c, ai, bi: (ai[p], c, 0)),
            pl.BlockSpec((1, cols, coords), lambda p, c, ai, bi: (bi[p], 0, 0)),
            pl.BlockSpec((1, cols, 1), lambda p, c, ai, bi: (p, 0, 0)),
        ],
        out_specs=pl.BlockSpec((1, 1, CHUNK), lambda p, c, ai, bi: (p, 0, c)),
    )
    return pl.pallas_call(
        _lse_kernel,
        grid_spec=spec,
        out_shape=jax.ShapeDtypeStruct((pairs, 1, rows), jnp.float32),
        interpret=interpret,
    )(a_ids, b_ids, a_pts, b_pts, v_col)


def _grad_kernel(a_ids, b_ids, a_ref, b_ref, v_ref, w_ref, o_ref):
    src = a_ref[0]
    tgt = b_ref[0]
    tile = lax.dot_general(src, tgt, (((1,), (1,)), ((), ())), preferred_element_type=jnp.float32)
    weights = jnp.exp(tile * INV_EPS + v_ref[0] + w_ref[0])
    mass = jnp.sum(weights, axis=1, keepdims=True)
    moved = jnp.dot(weights.astype(jnp.bfloat16), tgt, preferred_element_type=jnp.float32)
    o_ref[0] = mass * src.astype(jnp.float32) - moved


def pair_grad(a_ids, b_ids, a_pts, b_pts, v_row, w_col, interpret=False):
    pairs = a_ids.shape[0]
    rows = a_pts.shape[1]
    coords = a_pts.shape[2]
    cols = b_pts.shape[1]
    spec = pltpu.PrefetchScalarGridSpec(
        num_scalar_prefetch=2,
        grid=(pairs, rows // CHUNK),
        in_specs=[
            pl.BlockSpec((1, CHUNK, coords), lambda p, c, ai, bi: (ai[p], c, 0)),
            pl.BlockSpec((1, cols, coords), lambda p, c, ai, bi: (bi[p], 0, 0)),
            pl.BlockSpec((1, 1, cols), lambda p, c, ai, bi: (p, 0, 0)),
            pl.BlockSpec((1, CHUNK, 1), lambda p, c, ai, bi: (p, c, 0)),
        ],
        out_specs=pl.BlockSpec((1, CHUNK, coords), lambda p, c, ai, bi: (p, c, 0)),
    )
    return pl.pallas_call(
        _grad_kernel,
        grid_spec=spec,
        out_shape=jax.ShapeDtypeStruct((pairs, rows, coords), jnp.float32),
        interpret=interpret,
    )(a_ids, b_ids, a_pts, b_pts, v_row, w_col)


def grouped_lse(mask, values):
    masked = jnp.where(mask[:, :, None], values[None], EMPTY_LOG)
    peak_val = jnp.max(masked, axis=1)
    return peak_val + jnp.log(jnp.sum(jnp.exp(masked - peak_val[:, None]), axis=1))


def spread(block, axis, reach, has_sender):
    width = block.shape[0]
    index = lax.axis_index(axis)
    count = lax.axis_size(axis)
    parts = [block]
    pad = jnp.full((reach,) + block.shape[1:], EMPTY_LOG, block.dtype)
    for distance in range(-reach, reach + 1):
        if distance == 0:
            continue
        got = passed_along(block, axis, distance)
        valid = (index - distance >= 0) & (index - distance < count)
        got = jnp.where(valid, got, EMPTY_LOG)
        got = jnp.concatenate([pad, got, pad], axis=0)
        parts.append(lax.slice_in_dim(got, reach + distance, reach + distance + width, axis=0))
    parts = jnp.stack(parts)
    peak_val = jnp.max(parts, axis=0)
    return peak_val + jnp.log(jnp.sum(jnp.exp(parts - peak_val[None]), axis=0))


def gather_rows(row, axis):
    index = lax.axis_index(axis)
    count = lax.axis_size(axis)
    block = row
    step = 1
    while step < count:
        route = [(i, i ^ step) for i in range(count)]
        other = lax.ppermute(block, axis, route)
        upper = (index // step) % 2 == 1
        block = jnp.where(
            upper, jnp.concatenate([other, block], axis=0), jnp.concatenate([block, other], axis=0)
        )
        step *= 2
    return block


def body(src_points, tgt_points, src_log_mass, tgt_log_mass, near_pairs, target_slot):
    owned = tgt_points.shape[0]
    group_size = src_points.shape[0]
    gx_count = lax.axis_size("gx")
    gy_count = lax.axis_size("gy")
    gx_index = lax.axis_index("gx")
    gy_index = lax.axis_index("gy")
    source_local = jnp.clip(near_pairs[:, 0] - gx_index * group_size, 0, group_size - 1)
    matches = (
        near_pairs[:, 1][:, None] == jnp.arange(target_slot.shape[0], dtype=jnp.int32)[None, :]
    )
    slot_ids = jnp.sum(jnp.where(matches, target_slot[None, :], 0), axis=1)
    window_ids = (slot_ids // owned // gy_count - gx_index + 1) * owned + slot_ids % owned
    window_ids = jnp.clip(window_ids, 0, 3 * owned - 1)
    span_ids = jnp.clip(source_local - (gy_index - 2) * owned, 0, 5 * owned - 1)
    span_mask = span_ids[None, :] == jnp.arange(5 * owned, dtype=jnp.int32)[:, None]
    window_mask = window_ids[None, :] == jnp.arange(3 * owned, dtype=jnp.int32)[:, None]
    pair_src_sq = squares(src_points[source_local])
    window_pts, window_sq = fetch_points(tgt_points)
    pair_tgt_sq = window_sq[window_ids]
    window_mass = fetch_potential(tgt_log_mass)
    mass_pad = jnp.zeros((2 * owned,) + src_log_mass.shape[1:], src_log_mass.dtype)
    span_mass = lax.dynamic_slice_in_dim(
        jnp.concatenate([mass_pad, src_log_mass, mass_pad], axis=0), gy_index * owned, 5 * owned, 0
    )
    g_window = jnp.zeros((3 * owned, src_points.shape[1]), jnp.float32)
    for sweep_index in range(ITERS):
        v_row = (g_window[window_ids] - 0.5 * pair_tgt_sq) / EPSILON
        part = pair_lse(source_local, window_ids, src_points, window_pts, v_row[:, :, None])
        part = part[:, 0] - 0.5 * pair_src_sq / EPSILON
        rows_total = spread(grouped_lse(span_mask, part), "gy", 4 * owned, None)
        f_span = EPSILON * span_mass - EPSILON * rows_total
        v_col = (f_span[span_ids] - 0.5 * pair_src_sq) / EPSILON
        part = pair_lse(window_ids, source_local, window_pts, src_points, v_col[:, :, None])
        part = part[:, 0] - 0.5 * pair_tgt_sq / EPSILON
        cols_total = spread(grouped_lse(window_mask, part), "gx", 2 * owned, None)
        g_window = EPSILON * window_mass - EPSILON * cols_total
    f_pot = gather_rows(f_span[2 * owned : 3 * owned], "gy")
    g_local = g_window[owned : 2 * owned]
    v_row = (g_window[window_ids] - 0.5 * pair_tgt_sq) / EPSILON
    w_col = (f_span[span_ids] - 0.5 * pair_src_sq) / EPSILON
    contrib = pair_grad(
        source_local, window_ids, src_points, window_pts, v_row[:, None, :], w_col[:, :, None]
    )
    span_parts = jnp.sum(jnp.where(span_mask[:, :, None, None], contrib[None], 0.0), axis=1)
    grad = span_parts[2 * owned : 3 * owned]
    for distance in (1, 2):
        upper = passed_along(
            span_parts[(2 - distance) * owned : (3 - distance) * owned], "gy", -distance
        )
        lower = passed_along(
            span_parts[(2 + distance) * owned : (3 + distance) * owned], "gy", distance
        )
        grad = grad + upper + lower
    return (f_pot, g_local, grad)


def solution(mesh):
    in_specs = (
        P("gx", None, None),
        P(("gx", "gy"), None, None),
        P("gx", None),
        P(("gx", "gy"), None),
        P(("gx", "gy"), None),
        P(),
    )
    out_specs = (P("gx", None), P(("gx", "gy"), None), P(("gx", "gy"), None, None))
    return jax.shard_map(body, mesh=mesh, in_specs=in_specs, out_specs=out_specs, check_vma=False)
```

```python
import jax
import jax.numpy as jnp
from jax import lax
from jax.sharding import PartitionSpec as P
from jax.experimental import pallas as pl
from jax.experimental.pallas import tpu as pltpu

ITERS = 3


EMPTY_LOG = -1e30


def padded(block, sides, width):
    for axis, dim in sides:
        count = lax.axis_size(axis)
        forward = [(i, i + 1) for i in range(count - 1)]
        backward = [(target, source) for source, target in forward]
        low = lax.ppermute(
            lax.slice_in_dim(block, block.shape[dim] - width, None, axis=dim), axis, forward
        )
        high = lax.ppermute(lax.slice_in_dim(block, 0, width, axis=dim), axis, backward)
        block = jnp.concatenate([low, block, high], axis=dim)
    return block


def passed_along(block, axis, distance):
    devices = range(lax.axis_size(axis))
    route = [(i - distance, i) for i in devices if i - distance in devices]
    return lax.ppermute(block, axis, route)


def log_add(first, second):
    peak_val = jnp.maximum(first, second)
    return peak_val + jnp.log(jnp.exp(first - peak_val) + jnp.exp(second - peak_val))


def pick(table, position):
    return lax.dynamic_index_in_dim(table, position, 0, keepdims=False)


def cost_tile(src_rows, tgt_rows, src_sq, tgt_sq):
    inner = lax.dot_general(
        src_rows, tgt_rows, (((1,), (1,)), ((), ())), preferred_element_type=jnp.float32
    )
    return 0.5 * (src_sq[:, None] + tgt_sq[None, :]) - inner


def squares(points):
    return jnp.sum(jnp.square(points.astype(jnp.float32)), axis=-1)


def fetch_points(tgt_points):
    window_pts = padded(tgt_points, (("gx", 0),), tgt_points.shape[0])
    return (window_pts, squares(window_pts))


def fetch_potential(g_local):
    return padded(g_local, (("gx", 0),), g_local.shape[0])


EPSILON = 0.03
INV_EPS = 1.0 / EPSILON
CHUNK = 1024


def _lse_kernel(a_ids, b_ids, a_ref, b_ref, v_ref, o_ref):
    tile = lax.dot_general(
        b_ref[0], a_ref[0], (((1,), (1,)), ((), ())), preferred_element_type=jnp.float32
    )
    scores = tile * INV_EPS + jnp.transpose(v_ref[0])[:, :1]
    peak = jnp.max(scores, axis=0, keepdims=True)
    total = jnp.sum(jnp.exp(scores - peak), axis=0, keepdims=True)
    o_ref[0] = peak + jnp.log(total)


def pair_lse(a_ids, b_ids, a_pts, b_pts, v_rows, interpret=False):
    pairs = a_ids.shape[0]
    rows = a_pts.shape[1]
    coords = a_pts.shape[2]
    cols = b_pts.shape[1]
    spec = pltpu.PrefetchScalarGridSpec(
        num_scalar_prefetch=2,
        grid=(pairs, rows // CHUNK),
        in_specs=[
            pl.BlockSpec((1, CHUNK, coords), lambda p, c, ai, bi: (ai[p], c, 0)),
            pl.BlockSpec((1, cols, coords), lambda p, c, ai, bi: (bi[p], 0, 0)),
            pl.BlockSpec((1, 8, cols), lambda p, c, ai, bi: (p, 0, 0)),
        ],
        out_specs=pl.BlockSpec((1, 1, CHUNK), lambda p, c, ai, bi: (p, 0, c)),
    )
    return pl.pallas_call(
        _lse_kernel,
        grid_spec=spec,
        out_shape=jax.ShapeDtypeStruct((pairs, 1, rows), jnp.float32),
        interpret=interpret,
    )(a_ids, b_ids, a_pts, b_pts, v_rows)


def _grad_kernel(a_ids, b_ids, a_ref, b_ref, v_ref, w_ref, o_ref):
    src = a_ref[0]
    tgt = b_ref[0]
    tile = lax.dot_general(src, tgt, (((1,), (1,)), ((), ())), preferred_element_type=jnp.float32)
    weights = jnp.exp(tile * INV_EPS + v_ref[0] + w_ref[0])
    mass = jnp.sum(weights, axis=1, keepdims=True)
    moved = jnp.dot(weights.astype(jnp.bfloat16), tgt, preferred_element_type=jnp.float32)
    o_ref[0] = mass * src.astype(jnp.float32) - moved


def pair_grad(a_ids, b_ids, a_pts, b_pts, v_row, w_col, interpret=False):
    pairs = a_ids.shape[0]
    rows = a_pts.shape[1]
    coords = a_pts.shape[2]
    cols = b_pts.shape[1]
    spec = pltpu.PrefetchScalarGridSpec(
        num_scalar_prefetch=2,
        grid=(pairs, rows // CHUNK),
        in_specs=[
            pl.BlockSpec((1, CHUNK, coords), lambda p, c, ai, bi: (ai[p], c, 0)),
            pl.BlockSpec((1, cols, coords), lambda p, c, ai, bi: (bi[p], 0, 0)),
            pl.BlockSpec((1, 1, cols), lambda p, c, ai, bi: (p, 0, 0)),
            pl.BlockSpec((1, CHUNK, 1), lambda p, c, ai, bi: (p, c, 0)),
        ],
        out_specs=pl.BlockSpec((1, CHUNK, coords), lambda p, c, ai, bi: (p, c, 0)),
    )
    return pl.pallas_call(
        _grad_kernel,
        grid_spec=spec,
        out_shape=jax.ShapeDtypeStruct((pairs, rows, coords), jnp.float32),
        interpret=interpret,
    )(a_ids, b_ids, a_pts, b_pts, v_row, w_col)


def grouped_lse(mask, values):
    masked = jnp.where(mask[:, :, None], values[None], EMPTY_LOG)
    peak_val = jnp.max(masked, axis=1)
    return peak_val + jnp.log(jnp.sum(jnp.exp(masked - peak_val[:, None]), axis=1))


def spread(block, axis, reach, has_sender):
    width = block.shape[0]
    index = lax.axis_index(axis)
    count = lax.axis_size(axis)
    parts = [block]
    pad = jnp.full((reach,) + block.shape[1:], EMPTY_LOG, block.dtype)
    for distance in range(-reach, reach + 1):
        if distance == 0:
            continue
        got = passed_along(block, axis, distance)
        valid = (index - distance >= 0) & (index - distance < count)
        got = jnp.where(valid, got, EMPTY_LOG)
        got = jnp.concatenate([pad, got, pad], axis=0)
        parts.append(lax.slice_in_dim(got, reach + distance, reach + distance + width, axis=0))
    parts = jnp.stack(parts)
    peak_val = jnp.max(parts, axis=0)
    return peak_val + jnp.log(jnp.sum(jnp.exp(parts - peak_val[None]), axis=0))


def shifted(block, shift, width):
    reach = abs(shift) + width
    pad = jnp.full((reach,) + block.shape[1:], EMPTY_LOG, block.dtype)
    padded_block = jnp.concatenate([pad, block, pad], axis=0)
    return lax.slice_in_dim(padded_block, reach + shift, reach + shift + width, axis=0)


def received(block, axis, distance):
    index = lax.axis_index(axis)
    count = lax.axis_size(axis)
    got = passed_along(block, axis, distance)
    valid = (index - distance >= 0) & (index - distance < count)
    return jnp.where(valid, got, EMPTY_LOG)


def lse_stack(parts):
    parts = jnp.stack(parts)
    peak_val = jnp.max(parts, axis=0)
    return peak_val + jnp.log(jnp.sum(jnp.exp(parts - peak_val[None]), axis=0))


def spread_rows(block, axis, owned):
    index = lax.axis_index(axis)
    count = lax.axis_size(axis)
    edge = lax.ppermute(block, axis, [(0, 2), (count - 1, count - 3)])
    edge = jnp.where(
        index == 2, shifted(edge, 2 * owned, 5 * owned), shifted(edge, -2 * owned, 5 * owned)
    )
    edge = jnp.where((index == 2) | (index == count - 3), edge, EMPTY_LOG)
    first = lse_stack(
        [
            shifted(block, -owned, 7 * owned),
            shifted(received(block, axis, 1), 0, 7 * owned),
            shifted(received(block, axis, -1), -2 * owned, 7 * owned),
        ]
    )
    return lse_stack(
        [
            shifted(first, owned, 5 * owned),
            shifted(received(first, axis, 3), 4 * owned, 5 * owned),
            shifted(received(first, axis, -3), -2 * owned, 5 * owned),
            edge,
        ]
    )


def gather_rows(row, axis):
    index = lax.axis_index(axis)
    count = lax.axis_size(axis)
    block = row
    step = 1
    while step < count:
        route = [(i, i ^ step) for i in range(count)]
        other = lax.ppermute(block, axis, route)
        upper = (index // step) % 2 == 1
        block = jnp.where(
            upper, jnp.concatenate([other, block], axis=0), jnp.concatenate([block, other], axis=0)
        )
        step *= 2
    return block


def body(src_points, tgt_points, src_log_mass, tgt_log_mass, near_pairs, target_slot):
    owned = tgt_points.shape[0]
    group_size = src_points.shape[0]
    gx_count = lax.axis_size("gx")
    gy_count = lax.axis_size("gy")
    gx_index = lax.axis_index("gx")
    gy_index = lax.axis_index("gy")
    source_local = jnp.clip(near_pairs[:, 0] - gx_index * group_size, 0, group_size - 1)
    matches = (
        near_pairs[:, 1][:, None] == jnp.arange(target_slot.shape[0], dtype=jnp.int32)[None, :]
    )
    slot_ids = jnp.sum(jnp.where(matches, target_slot[None, :], 0), axis=1)
    window_ids = (slot_ids // owned // gy_count - gx_index + 1) * owned + slot_ids % owned
    window_ids = jnp.clip(window_ids, 0, 3 * owned - 1)
    span_ids = jnp.clip(source_local - (gy_index - 2) * owned, 0, 5 * owned - 1)
    span_mask = span_ids[None, :] == jnp.arange(5 * owned, dtype=jnp.int32)[:, None]
    window_mask = window_ids[None, :] == jnp.arange(3 * owned, dtype=jnp.int32)[:, None]
    pair_src_sq = squares(src_points[source_local])
    window_pts, window_sq = fetch_points(tgt_points)
    pair_tgt_sq = window_sq[window_ids]
    window_mass = fetch_potential(tgt_log_mass)
    mass_pad = jnp.zeros((2 * owned,) + src_log_mass.shape[1:], src_log_mass.dtype)
    span_mass = lax.dynamic_slice_in_dim(
        jnp.concatenate([mass_pad, src_log_mass, mass_pad], axis=0), gy_index * owned, 5 * owned, 0
    )
    g_window = jnp.zeros((3 * owned, src_points.shape[1]), jnp.float32)
    for sweep_index in range(ITERS):
        v_row = (g_window[window_ids] - 0.5 * pair_tgt_sq) / EPSILON
        part = pair_lse(source_local, window_ids, src_points, window_pts, jnp.broadcast_to(v_row[:, None, :], (v_row.shape[0], 8, v_row.shape[1])))
        part = part[:, 0] - 0.5 * pair_src_sq / EPSILON
        rows_total = spread_rows(grouped_lse(span_mask, part), "gy", owned)
        f_span = EPSILON * span_mass - EPSILON * rows_total
        v_col = (f_span[span_ids] - 0.5 * pair_src_sq) / EPSILON
        part = pair_lse(window_ids, source_local, window_pts, src_points, jnp.broadcast_to(v_col[:, None, :], (v_col.shape[0], 8, v_col.shape[1])))
        part = part[:, 0] - 0.5 * pair_tgt_sq / EPSILON
        cols_total = spread(grouped_lse(window_mask, part), "gx", 2 * owned, None)
        g_window = EPSILON * window_mass - EPSILON * cols_total
    f_pot = gather_rows(f_span[2 * owned : 3 * owned], "gy")
    g_local = g_window[owned : 2 * owned]
    v_row = (g_window[window_ids] - 0.5 * pair_tgt_sq) / EPSILON
    w_col = (f_span[span_ids] - 0.5 * pair_src_sq) / EPSILON
    contrib = pair_grad(
        source_local, window_ids, src_points, window_pts, v_row[:, None, :], w_col[:, :, None]
    )
    span_parts = jnp.sum(jnp.where(span_mask[:, :, None, None], contrib[None], 0.0), axis=1)
    grad = span_parts[2 * owned : 3 * owned]
    for distance in (1, 2):
        upper = passed_along(
            span_parts[(2 - distance) * owned : (3 - distance) * owned], "gy", -distance
        )
        lower = passed_along(
            span_parts[(2 + distance) * owned : (3 + distance) * owned], "gy", distance
        )
        grad = grad + upper + lower
    return (f_pot, g_local, grad)


def solution(mesh):
    in_specs = (
        P("gx", None, None),
        P(("gx", "gy"), None, None),
        P("gx", None),
        P(("gx", "gy"), None),
        P(("gx", "gy"), None),
        P(),
    )
    out_specs = (P("gx", None), P(("gx", "gy"), None), P(("gx", "gy"), None, None))
    return jax.shard_map(body, mesh=mesh, in_specs=in_specs, out_specs=out_specs, check_vma=False)
```

```python
import jax
import jax.numpy as jnp
from jax import lax
from jax.sharding import PartitionSpec as P
from jax.experimental import pallas as pl
from jax.experimental.pallas import tpu as pltpu

ITERS = 3


EMPTY_LOG = -1e30


def padded(block, sides, width):
    for axis, dim in sides:
        count = lax.axis_size(axis)
        forward = [(i, i + 1) for i in range(count - 1)]
        backward = [(target, source) for source, target in forward]
        low = lax.ppermute(
            lax.slice_in_dim(block, block.shape[dim] - width, None, axis=dim), axis, forward
        )
        high = lax.ppermute(lax.slice_in_dim(block, 0, width, axis=dim), axis, backward)
        block = jnp.concatenate([low, block, high], axis=dim)
    return block


def passed_along(block, axis, distance):
    devices = range(lax.axis_size(axis))
    route = [(i - distance, i) for i in devices if i - distance in devices]
    return lax.ppermute(block, axis, route)


def squares(points):
    return jnp.sum(jnp.square(points.astype(jnp.float32)), axis=-1)


def fetch_points(tgt_points):
    window_pts = padded(tgt_points, (("gx", 0),), tgt_points.shape[0])
    return (window_pts, squares(window_pts))


def fetch_potential(g_local):
    return padded(g_local, (("gx", 0),), g_local.shape[0])


EPSILON = 0.03
INV_EPS = 1.0 / EPSILON
CHUNK = 1024
KERNEL_PARAMS = pltpu.CompilerParams()


def _lse_kernel(a_ids, b_ids, a_ref, b_ref, v_ref, o_ref):
    tile = lax.dot_general(
        b_ref[0], a_ref[0], (((1,), (1,)), ((), ())), preferred_element_type=jnp.float32
    )
    scores = tile * INV_EPS + jnp.transpose(v_ref[0])[:, :1]
    peak = jnp.max(scores, axis=0, keepdims=True)
    total = jnp.sum(jnp.exp(scores - peak), axis=0, keepdims=True)
    o_ref[0] = peak + jnp.log(total)


def pair_lse(a_ids, b_ids, a_pts, b_pts, v_rows, interpret=False):
    pairs = a_ids.shape[0]
    rows = a_pts.shape[1]
    coords = a_pts.shape[2]
    cols = b_pts.shape[1]
    spec = pltpu.PrefetchScalarGridSpec(
        num_scalar_prefetch=2,
        grid=(pairs, rows // CHUNK),
        in_specs=[
            pl.BlockSpec((1, CHUNK, coords), lambda p, c, ai, bi: (ai[p], c, 0)),
            pl.BlockSpec((1, cols, coords), lambda p, c, ai, bi: (bi[p], 0, 0)),
            pl.BlockSpec((1, 8, cols), lambda p, c, ai, bi: (p, 0, 0)),
        ],
        out_specs=pl.BlockSpec((1, 1, CHUNK), lambda p, c, ai, bi: (p, 0, c)),
    )
    return pl.pallas_call(
        _lse_kernel,
        grid_spec=spec,
        out_shape=jax.ShapeDtypeStruct((pairs, 1, rows), jnp.float32),
        interpret=interpret,
        compiler_params=KERNEL_PARAMS,
    )(a_ids, b_ids, a_pts, b_pts, v_rows)


def _grad_kernel(a_ids, b_ids, a_ref, b_ref, v_ref, w_ref, o_ref):
    src = a_ref[0]
    tgt = b_ref[0]
    tile = lax.dot_general(src, tgt, (((1,), (1,)), ((), ())), preferred_element_type=jnp.float32)
    weights = jnp.exp(tile * INV_EPS + v_ref[0] + w_ref[0])
    mass = jnp.sum(weights, axis=1, keepdims=True)
    moved = jnp.dot(weights.astype(jnp.bfloat16), tgt, preferred_element_type=jnp.float32)
    o_ref[0] = mass * src.astype(jnp.float32) - moved


def pair_grad(a_ids, b_ids, a_pts, b_pts, v_row, w_col, interpret=False):
    pairs = a_ids.shape[0]
    rows = a_pts.shape[1]
    coords = a_pts.shape[2]
    cols = b_pts.shape[1]
    spec = pltpu.PrefetchScalarGridSpec(
        num_scalar_prefetch=2,
        grid=(pairs, rows // CHUNK),
        in_specs=[
            pl.BlockSpec((1, CHUNK, coords), lambda p, c, ai, bi: (ai[p], c, 0)),
            pl.BlockSpec((1, cols, coords), lambda p, c, ai, bi: (bi[p], 0, 0)),
            pl.BlockSpec((1, 1, cols), lambda p, c, ai, bi: (p, 0, 0)),
            pl.BlockSpec((1, CHUNK, 1), lambda p, c, ai, bi: (p, c, 0)),
        ],
        out_specs=pl.BlockSpec((1, CHUNK, coords), lambda p, c, ai, bi: (p, c, 0)),
    )
    return pl.pallas_call(
        _grad_kernel,
        grid_spec=spec,
        out_shape=jax.ShapeDtypeStruct((pairs, rows, coords), jnp.float32),
        interpret=interpret,
        compiler_params=KERNEL_PARAMS,
    )(a_ids, b_ids, a_pts, b_pts, v_row, w_col)


def grouped_lse(mask, values):
    masked = jnp.where(mask[:, :, None], values[None], EMPTY_LOG)
    peak_val = jnp.max(masked, axis=1)
    return peak_val + jnp.log(jnp.sum(jnp.exp(masked - peak_val[:, None]), axis=1))


def spread(block, axis, reach):
    width = block.shape[0]
    index = lax.axis_index(axis)
    count = lax.axis_size(axis)
    parts = [block]
    pad = jnp.full((reach,) + block.shape[1:], EMPTY_LOG, block.dtype)
    for distance in range(-reach, reach + 1):
        if distance == 0:
            continue
        got = passed_along(block, axis, distance)
        valid = (index - distance >= 0) & (index - distance < count)
        got = jnp.where(valid, got, EMPTY_LOG)
        got = jnp.concatenate([pad, got, pad], axis=0)
        parts.append(lax.slice_in_dim(got, reach + distance, reach + distance + width, axis=0))
    parts = jnp.stack(parts)
    peak_val = jnp.max(parts, axis=0)
    return peak_val + jnp.log(jnp.sum(jnp.exp(parts - peak_val[None]), axis=0))


def shifted(block, shift, width):
    reach = abs(shift) + width
    pad = jnp.full((reach,) + block.shape[1:], EMPTY_LOG, block.dtype)
    padded_block = jnp.concatenate([pad, block, pad], axis=0)
    return lax.slice_in_dim(padded_block, reach + shift, reach + shift + width, axis=0)


def received(block, axis, distance):
    index = lax.axis_index(axis)
    count = lax.axis_size(axis)
    got = passed_along(block, axis, distance)
    valid = (index - distance >= 0) & (index - distance < count)
    return jnp.where(valid, got, EMPTY_LOG)


def lse_stack(parts):
    parts = jnp.stack(parts)
    peak_val = jnp.max(parts, axis=0)
    return peak_val + jnp.log(jnp.sum(jnp.exp(parts - peak_val[None]), axis=0))


def spread_rows(block, axis, owned):
    index = lax.axis_index(axis)
    count = lax.axis_size(axis)
    edge = lax.ppermute(block, axis, [(0, 2), (count - 1, count - 3)])
    edge = jnp.where(
        index == 2, shifted(edge, 2 * owned, 5 * owned), shifted(edge, -2 * owned, 5 * owned)
    )
    edge = jnp.where((index == 2) | (index == count - 3), edge, EMPTY_LOG)
    first = lse_stack(
        [
            shifted(block, -owned, 7 * owned),
            shifted(received(block, axis, 1), 0, 7 * owned),
            shifted(received(block, axis, -1), -2 * owned, 7 * owned),
        ]
    )
    return lse_stack(
        [
            shifted(first, owned, 5 * owned),
            shifted(received(first, axis, 3), 4 * owned, 5 * owned),
            shifted(received(first, axis, -3), -2 * owned, 5 * owned),
            edge,
        ]
    )


def gather_rows(row, axis):
    index = lax.axis_index(axis)
    count = lax.axis_size(axis)
    block = row
    step = 1
    while step < count:
        route = [(i, i ^ step) for i in range(count)]
        other = lax.ppermute(block, axis, route)
        upper = (index // step) % 2 == 1
        block = jnp.where(
            upper, jnp.concatenate([other, block], axis=0), jnp.concatenate([block, other], axis=0)
        )
        step *= 2
    return block


def body(src_points, tgt_points, src_log_mass, tgt_log_mass, near_pairs, target_slot):
    owned = tgt_points.shape[0]
    group_size = src_points.shape[0]
    gy_count = lax.axis_size("gy")
    gx_index = lax.axis_index("gx")
    gy_index = lax.axis_index("gy")
    source_local = jnp.clip(near_pairs[:, 0] - gx_index * group_size, 0, group_size - 1)
    matches = (
        near_pairs[:, 1][:, None] == jnp.arange(target_slot.shape[0], dtype=jnp.int32)[None, :]
    )
    slot_ids = jnp.sum(jnp.where(matches, target_slot[None, :], 0), axis=1)
    window_ids = (slot_ids // owned // gy_count - gx_index + 1) * owned + slot_ids % owned
    window_ids = jnp.clip(window_ids, 0, 3 * owned - 1)
    span_ids = jnp.clip(source_local - (gy_index - 2) * owned, 0, 5 * owned - 1)
    span_mask = span_ids[None, :] == jnp.arange(5 * owned, dtype=jnp.int32)[:, None]
    window_mask = window_ids[None, :] == jnp.arange(3 * owned, dtype=jnp.int32)[:, None]
    pair_src_sq = squares(src_points[source_local])
    window_pts, window_sq = fetch_points(tgt_points)
    pair_tgt_sq = window_sq[window_ids]
    window_mass = fetch_potential(tgt_log_mass)
    mass_pad = jnp.zeros((2 * owned,) + src_log_mass.shape[1:], src_log_mass.dtype)
    span_mass = lax.dynamic_slice_in_dim(
        jnp.concatenate([mass_pad, src_log_mass, mass_pad], axis=0), gy_index * owned, 5 * owned, 0
    )
    g_window = jnp.zeros((3 * owned, src_points.shape[1]), jnp.float32)
    for _ in range(ITERS):
        v_row = (g_window[window_ids] - 0.5 * pair_tgt_sq) / EPSILON
        part = pair_lse(source_local, window_ids, src_points, window_pts, jnp.broadcast_to(v_row[:, None, :], (v_row.shape[0], 8, v_row.shape[1])))
        part = part[:, 0] - 0.5 * pair_src_sq / EPSILON
        rows_total = spread_rows(grouped_lse(span_mask, part), "gy", owned)
        f_span = EPSILON * span_mass - EPSILON * rows_total
        v_col = (f_span[span_ids] - 0.5 * pair_src_sq) / EPSILON
        part = pair_lse(
            window_ids, source_local, window_pts, src_points,
            jnp.broadcast_to(v_col[:, None, :], (v_col.shape[0], 8, v_col.shape[1])),
        )
        part = part[:, 0] - 0.5 * pair_tgt_sq / EPSILON
        cols_total = spread(grouped_lse(window_mask, part), "gx", 2 * owned)
        g_window = EPSILON * window_mass - EPSILON * cols_total
    f_pot = gather_rows(f_span[2 * owned : 3 * owned], "gy")
    g_local = g_window[owned : 2 * owned]
    v_row = (g_window[window_ids] - 0.5 * pair_tgt_sq) / EPSILON
    w_col = (f_span[span_ids] - 0.5 * pair_src_sq) / EPSILON
    contrib = pair_grad(
        source_local, window_ids, src_points, window_pts, v_row[:, None, :], w_col[:, :, None]
    )
    span_parts = jnp.sum(jnp.where(span_mask[:, :, None, None], contrib[None], 0.0), axis=1)
    grad = span_parts[2 * owned : 3 * owned]
    for distance in (1, 2):
        upper = passed_along(
            span_parts[(2 - distance) * owned : (3 - distance) * owned], "gy", -distance
        )
        lower = passed_along(
            span_parts[(2 + distance) * owned : (3 + distance) * owned], "gy", distance
        )
        grad = grad + upper + lower
    return (f_pot, g_local, grad)


def solution(mesh):
    in_specs = (
        P("gx", None, None),
        P(("gx", "gy"), None, None),
        P("gx", None),
        P(("gx", "gy"), None),
        P(("gx", "gy"), None),
        P(),
    )
    out_specs = (P("gx", None), P(("gx", "gy"), None), P(("gx", "gy"), None, None))

    return jax.shard_map(body, mesh=mesh, in_specs=in_specs, out_specs=out_specs, check_vma=False)
```

```python
import jax
import jax.numpy as jnp
from jax import lax
from jax.sharding import PartitionSpec as P
from jax.experimental import pallas as pl
from jax.experimental.pallas import tpu as pltpu

ITERS = 3


EMPTY_LOG = -1e30


def padded(block, sides, width):
    for axis, dim in sides:
        count = lax.axis_size(axis)
        forward = [(i, i + 1) for i in range(count - 1)]
        backward = [(target, source) for source, target in forward]
        low = lax.ppermute(
            lax.slice_in_dim(block, block.shape[dim] - width, None, axis=dim), axis, forward
        )
        high = lax.ppermute(lax.slice_in_dim(block, 0, width, axis=dim), axis, backward)
        block = jnp.concatenate([low, block, high], axis=dim)
    return block


def passed_along(block, axis, distance):
    devices = range(lax.axis_size(axis))
    route = [(i - distance, i) for i in devices if i - distance in devices]
    return lax.ppermute(block, axis, route)


def squares(points):
    return jnp.sum(jnp.square(points.astype(jnp.float32)), axis=-1)


def fetch_points(tgt_points):
    window_pts = padded(tgt_points, (("gx", 0),), tgt_points.shape[0])
    return (window_pts, squares(window_pts))


def fetch_potential(g_local):
    return padded(g_local, (("gx", 0),), g_local.shape[0])


EPSILON = 0.03
INV_EPS = 1.0 / EPSILON
CHUNK = 1024
KERNEL_PARAMS = pltpu.CompilerParams()


def _lse_kernel(a_ids, b_ids, a_ref, b_ref, v_ref, o_ref):
    tile = lax.dot_general(
        b_ref[0], a_ref[0], (((1,), (1,)), ((), ())), preferred_element_type=jnp.float32
    )
    scores = tile * INV_EPS + jnp.transpose(v_ref[0])[:, :1]
    peak = jnp.max(scores, axis=0, keepdims=True)
    total = jnp.sum(jnp.exp(scores - peak), axis=0, keepdims=True)
    o_ref[0] = peak + jnp.log(total)


def pair_lse(a_ids, b_ids, a_pts, b_pts, v_rows, interpret=False):
    pairs = a_ids.shape[0]
    rows = a_pts.shape[1]
    coords = a_pts.shape[2]
    cols = b_pts.shape[1]
    spec = pltpu.PrefetchScalarGridSpec(
        num_scalar_prefetch=2,
        grid=(pairs, rows // CHUNK),
        in_specs=[
            pl.BlockSpec((1, CHUNK, coords), lambda p, c, ai, bi: (ai[p], c, 0)),
            pl.BlockSpec((1, cols, coords), lambda p, c, ai, bi: (bi[p], 0, 0)),
            pl.BlockSpec((1, 8, cols), lambda p, c, ai, bi: (p, 0, 0)),
        ],
        out_specs=pl.BlockSpec((1, 1, CHUNK), lambda p, c, ai, bi: (p, 0, c)),
    )
    return pl.pallas_call(
        _lse_kernel,
        grid_spec=spec,
        out_shape=jax.ShapeDtypeStruct((pairs, 1, rows), jnp.float32),
        interpret=interpret,
        compiler_params=KERNEL_PARAMS,
    )(a_ids, b_ids, a_pts, b_pts, v_rows)


def _grad_kernel(a_ids, b_ids, a_ref, b_ref, v_ref, w_ref, o_ref):
    src = a_ref[0]
    tgt = b_ref[0]
    tile = lax.dot_general(src, tgt, (((1,), (1,)), ((), ())), preferred_element_type=jnp.float32)
    weights = jnp.exp(tile * INV_EPS + v_ref[0] + w_ref[0])
    mass = jnp.sum(weights, axis=1, keepdims=True)
    moved = jnp.dot(weights.astype(jnp.bfloat16), tgt, preferred_element_type=jnp.float32)
    o_ref[0] = mass * src.astype(jnp.float32) - moved


def pair_grad(a_ids, b_ids, a_pts, b_pts, v_row, w_col, interpret=False):
    pairs = a_ids.shape[0]
    rows = a_pts.shape[1]
    coords = a_pts.shape[2]
    cols = b_pts.shape[1]
    spec = pltpu.PrefetchScalarGridSpec(
        num_scalar_prefetch=2,
        grid=(pairs, rows // CHUNK),
        in_specs=[
            pl.BlockSpec((1, CHUNK, coords), lambda p, c, ai, bi: (ai[p], c, 0)),
            pl.BlockSpec((1, cols, coords), lambda p, c, ai, bi: (bi[p], 0, 0)),
            pl.BlockSpec((1, 1, cols), lambda p, c, ai, bi: (p, 0, 0)),
            pl.BlockSpec((1, CHUNK, 1), lambda p, c, ai, bi: (p, c, 0)),
        ],
        out_specs=pl.BlockSpec((1, CHUNK, coords), lambda p, c, ai, bi: (p, c, 0)),
    )
    return pl.pallas_call(
        _grad_kernel,
        grid_spec=spec,
        out_shape=jax.ShapeDtypeStruct((pairs, rows, coords), jnp.float32),
        interpret=interpret,
        compiler_params=KERNEL_PARAMS,
    )(a_ids, b_ids, a_pts, b_pts, v_row, w_col)


def grouped_lse(mask, values):
    masked = jnp.where(mask[:, :, None], values[None], EMPTY_LOG)
    peak_val = jnp.max(masked, axis=1)
    return peak_val + jnp.log(jnp.sum(jnp.exp(masked - peak_val[:, None]), axis=1))


def spread(block, axis, reach):
    width = block.shape[0]
    index = lax.axis_index(axis)
    count = lax.axis_size(axis)
    parts = [block]
    pad = jnp.full((reach,) + block.shape[1:], EMPTY_LOG, block.dtype)
    for distance in range(-reach, reach + 1):
        if distance == 0:
            continue
        got = passed_along(block, axis, distance)
        valid = (index - distance >= 0) & (index - distance < count)
        got = jnp.where(valid, got, EMPTY_LOG)
        got = jnp.concatenate([pad, got, pad], axis=0)
        parts.append(lax.slice_in_dim(got, reach + distance, reach + distance + width, axis=0))
    parts = jnp.stack(parts)
    peak_val = jnp.max(parts, axis=0)
    return peak_val + jnp.log(jnp.sum(jnp.exp(parts - peak_val[None]), axis=0))


def shifted(block, shift, width):
    reach = abs(shift) + width
    pad = jnp.full((reach,) + block.shape[1:], EMPTY_LOG, block.dtype)
    padded_block = jnp.concatenate([pad, block, pad], axis=0)
    return lax.slice_in_dim(padded_block, reach + shift, reach + shift + width, axis=0)


def received(block, axis, distance):
    index = lax.axis_index(axis)
    count = lax.axis_size(axis)
    got = passed_along(block, axis, distance)
    valid = (index - distance >= 0) & (index - distance < count)
    return jnp.where(valid, got, EMPTY_LOG)


def lse_stack(parts):
    parts = jnp.stack(parts)
    peak_val = jnp.max(parts, axis=0)
    return peak_val + jnp.log(jnp.sum(jnp.exp(parts - peak_val[None]), axis=0))


def spread_rows(block, axis, owned):
    index = lax.axis_index(axis)
    count = lax.axis_size(axis)
    edge = lax.ppermute(block, axis, [(0, 2), (count - 1, count - 3)])
    edge = jnp.where(
        index == 2, shifted(edge, 2 * owned, 5 * owned), shifted(edge, -2 * owned, 5 * owned)
    )
    edge = jnp.where((index == 2) | (index == count - 3), edge, EMPTY_LOG)
    first = lse_stack(
        [
            shifted(block, -owned, 7 * owned),
            shifted(received(block, axis, 1), 0, 7 * owned),
            shifted(received(block, axis, -1), -2 * owned, 7 * owned),
        ]
    )
    return lse_stack(
        [
            shifted(first, owned, 5 * owned),
            shifted(received(first, axis, 3), 4 * owned, 5 * owned),
            shifted(received(first, axis, -3), -2 * owned, 5 * owned),
            edge,
        ]
    )


def body(src_points, tgt_points, src_log_mass, tgt_log_mass, near_pairs, target_slot):
    owned = tgt_points.shape[0]
    group_size = src_points.shape[0]
    gy_count = lax.axis_size("gy")
    gx_index = lax.axis_index("gx")
    gy_index = lax.axis_index("gy")
    source_local = jnp.clip(near_pairs[:, 0] - gx_index * group_size, 0, group_size - 1)
    matches = (
        near_pairs[:, 1][:, None] == jnp.arange(target_slot.shape[0], dtype=jnp.int32)[None, :]
    )
    slot_ids = jnp.sum(jnp.where(matches, target_slot[None, :], 0), axis=1)
    window_ids = (slot_ids // owned // gy_count - gx_index + 1) * owned + slot_ids % owned
    window_ids = jnp.clip(window_ids, 0, 3 * owned - 1)
    span_ids = jnp.clip(source_local - (gy_index - 2) * owned, 0, 5 * owned - 1)
    span_mask = span_ids[None, :] == jnp.arange(5 * owned, dtype=jnp.int32)[:, None]
    window_mask = window_ids[None, :] == jnp.arange(3 * owned, dtype=jnp.int32)[:, None]
    pair_src_sq = squares(src_points[source_local])
    window_pts, window_sq = fetch_points(tgt_points)
    pair_tgt_sq = window_sq[window_ids]
    window_mass = fetch_potential(tgt_log_mass)
    mass_pad = jnp.zeros((2 * owned,) + src_log_mass.shape[1:], src_log_mass.dtype)
    span_mass = lax.dynamic_slice_in_dim(
        jnp.concatenate([mass_pad, src_log_mass, mass_pad], axis=0), gy_index * owned, 5 * owned, 0
    )
    g_window = jnp.zeros((3 * owned, src_points.shape[1]), jnp.float32)
    for _ in range(ITERS):
        v_row = (g_window[window_ids] - 0.5 * pair_tgt_sq) / EPSILON
        part = pair_lse(source_local, window_ids, src_points, window_pts, jnp.broadcast_to(v_row[:, None, :], (v_row.shape[0], 8, v_row.shape[1])))
        part = part[:, 0] - 0.5 * pair_src_sq / EPSILON
        rows_total = spread_rows(grouped_lse(span_mask, part), "gy", owned)
        f_span = EPSILON * span_mass - EPSILON * rows_total
        v_col = (f_span[span_ids] - 0.5 * pair_src_sq) / EPSILON
        part = pair_lse(
            window_ids, source_local, window_pts, src_points,
            jnp.broadcast_to(v_col[:, None, :], (v_col.shape[0], 8, v_col.shape[1])),
        )
        part = part[:, 0] - 0.5 * pair_tgt_sq / EPSILON
        cols_total = spread(grouped_lse(window_mask, part), "gx", 2 * owned)
        g_window = EPSILON * window_mass - EPSILON * cols_total
    f_rows = jnp.zeros((group_size,) + f_span.shape[1:], f_span.dtype)
    f_rows = lax.dynamic_update_slice_in_dim(
        f_rows, f_span[2 * owned : 3 * owned], gy_index * owned, 0
    )
    f_pot = lax.psum(f_rows, "gy")
    g_local = g_window[owned : 2 * owned]
    v_row = (g_window[window_ids] - 0.5 * pair_tgt_sq) / EPSILON
    w_col = (f_span[span_ids] - 0.5 * pair_src_sq) / EPSILON
    contrib = pair_grad(
        source_local, window_ids, src_points, window_pts, v_row[:, None, :], w_col[:, :, None]
    )
    span_parts = jnp.sum(jnp.where(span_mask[:, :, None, None], contrib[None], 0.0), axis=1)
    grad = span_parts[2 * owned : 3 * owned]
    for distance in (1, 2):
        upper = passed_along(
            span_parts[(2 - distance) * owned : (3 - distance) * owned], "gy", -distance
        )
        lower = passed_along(
            span_parts[(2 + distance) * owned : (3 + distance) * owned], "gy", distance
        )
        grad = grad + upper + lower
    return (f_pot, g_local, grad)


def solution(mesh):
    in_specs = (
        P("gx", None, None),
        P(("gx", "gy"), None, None),
        P("gx", None),
        P(("gx", "gy"), None),
        P(("gx", "gy"), None),
        P(),
    )
    out_specs = (P("gx", None), P(("gx", "gy"), None), P(("gx", "gy"), None, None))

    return jax.shard_map(body, mesh=mesh, in_specs=in_specs, out_specs=out_specs, check_vma=False)
```

```python
import jax
import jax.numpy as jnp
from jax import lax
from jax.sharding import PartitionSpec as P
from jax.experimental import pallas as pl
from jax.experimental.pallas import tpu as pltpu

ITERS = 3


EMPTY_LOG = -1e30


def padded(block, sides, width):
    for axis, dim in sides:
        count = lax.axis_size(axis)
        forward = [(i, i + 1) for i in range(count - 1)]
        backward = [(target, source) for source, target in forward]
        low = lax.ppermute(
            lax.slice_in_dim(block, block.shape[dim] - width, None, axis=dim), axis, forward
        )
        high = lax.ppermute(lax.slice_in_dim(block, 0, width, axis=dim), axis, backward)
        block = jnp.concatenate([low, block, high], axis=dim)
    return block


def passed_along(block, axis, distance):
    devices = range(lax.axis_size(axis))
    route = [(i - distance, i) for i in devices if i - distance in devices]
    return lax.ppermute(block, axis, route)


def squares(points):
    return jnp.sum(jnp.square(points.astype(jnp.float32)), axis=-1)


def fetch_points(tgt_points):
    window_pts = padded(tgt_points, (("gx", 0),), tgt_points.shape[0])
    return (window_pts, squares(window_pts))


def fetch_potential(g_local):
    return padded(g_local, (("gx", 0),), g_local.shape[0])


EPSILON = 0.03
INV_EPS = 1.0 / EPSILON
CHUNK = 1024
KERNEL_PARAMS = pltpu.CompilerParams()


def _lse_kernel(a_ids, b_ids, a_ref, b_ref, v_ref, o_ref):
    tile = lax.dot_general(
        b_ref[0], a_ref[0], (((1,), (1,)), ((), ())), preferred_element_type=jnp.float32
    )
    scores = tile * INV_EPS + jnp.transpose(v_ref[0])[:, :1]
    peak = jnp.max(scores, axis=0, keepdims=True)
    total = jnp.sum(jnp.exp(scores - peak), axis=0, keepdims=True)
    o_ref[0] = peak + jnp.log(total)


def pair_lse(a_ids, b_ids, a_pts, b_pts, v_rows, interpret=False):
    pairs = a_ids.shape[0]
    rows = a_pts.shape[1]
    coords = a_pts.shape[2]
    cols = b_pts.shape[1]
    spec = pltpu.PrefetchScalarGridSpec(
        num_scalar_prefetch=2,
        grid=(pairs, rows // CHUNK),
        in_specs=[
            pl.BlockSpec((1, CHUNK, coords), lambda p, c, ai, bi: (ai[p], c, 0)),
            pl.BlockSpec((1, cols, coords), lambda p, c, ai, bi: (bi[p], 0, 0)),
            pl.BlockSpec((1, 8, cols), lambda p, c, ai, bi: (p, 0, 0)),
        ],
        out_specs=pl.BlockSpec((1, 1, CHUNK), lambda p, c, ai, bi: (p, 0, c)),
    )
    return pl.pallas_call(
        _lse_kernel,
        grid_spec=spec,
        out_shape=jax.ShapeDtypeStruct((pairs, 1, rows), jnp.float32),
        interpret=interpret,
        compiler_params=KERNEL_PARAMS,
    )(a_ids, b_ids, a_pts, b_pts, v_rows)


def _grad_kernel(a_ids, b_ids, a_ref, b_ref, v_ref, w_ref, o_ref):
    src = a_ref[0]
    tgt = b_ref[0]
    tile = lax.dot_general(src, tgt, (((1,), (1,)), ((), ())), preferred_element_type=jnp.float32)
    weights = jnp.exp(tile * INV_EPS + v_ref[0] + w_ref[0])
    mass = jnp.sum(weights, axis=1, keepdims=True)
    moved = jnp.dot(weights.astype(jnp.bfloat16), tgt, preferred_element_type=jnp.float32)
    o_ref[0] = mass * src.astype(jnp.float32) - moved


def pair_grad(a_ids, b_ids, a_pts, b_pts, v_row, w_col, interpret=False):
    pairs = a_ids.shape[0]
    rows = a_pts.shape[1]
    coords = a_pts.shape[2]
    cols = b_pts.shape[1]
    spec = pltpu.PrefetchScalarGridSpec(
        num_scalar_prefetch=2,
        grid=(pairs, rows // CHUNK),
        in_specs=[
            pl.BlockSpec((1, CHUNK, coords), lambda p, c, ai, bi: (ai[p], c, 0)),
            pl.BlockSpec((1, cols, coords), lambda p, c, ai, bi: (bi[p], 0, 0)),
            pl.BlockSpec((1, 1, cols), lambda p, c, ai, bi: (p, 0, 0)),
            pl.BlockSpec((1, CHUNK, 1), lambda p, c, ai, bi: (p, c, 0)),
        ],
        out_specs=pl.BlockSpec((1, CHUNK, coords), lambda p, c, ai, bi: (p, c, 0)),
    )
    return pl.pallas_call(
        _grad_kernel,
        grid_spec=spec,
        out_shape=jax.ShapeDtypeStruct((pairs, rows, coords), jnp.float32),
        interpret=interpret,
        compiler_params=KERNEL_PARAMS,
    )(a_ids, b_ids, a_pts, b_pts, v_row, w_col)


def grouped_lse(mask, values):
    masked = jnp.where(mask[:, :, None], values[None], EMPTY_LOG)
    peak_val = jnp.max(masked, axis=1)
    return peak_val + jnp.log(jnp.sum(jnp.exp(masked - peak_val[:, None]), axis=1))


def spread(block, axis, reach):
    width = block.shape[0]
    index = lax.axis_index(axis)
    count = lax.axis_size(axis)
    parts = [block]
    pad = jnp.full((reach,) + block.shape[1:], EMPTY_LOG, block.dtype)
    far = [reach, -reach] if count == 2 * reach else []
    for distance in range(-reach, reach + 1):
        if distance == 0 or distance in far:
            continue
        got = passed_along(block, axis, distance)
        valid = (index - distance >= 0) & (index - distance < count)
        got = jnp.where(valid, got, EMPTY_LOG)
        got = jnp.concatenate([pad, got, pad], axis=0)
        parts.append(lax.slice_in_dim(got, reach + distance, reach + distance + width, axis=0))
    if far:
        got = lax.ppermute(block, axis, [(i, (i + reach) % count) for i in range(count)])
        got = jnp.concatenate([pad, got, pad], axis=0)
        upper = lax.slice_in_dim(got, 2 * reach, 2 * reach + width, axis=0)
        lower = lax.slice_in_dim(got, 0, width, axis=0)
        parts.append(jnp.where(index >= reach, upper, lower))
    parts = jnp.stack(parts)
    peak_val = jnp.max(parts, axis=0)
    return peak_val + jnp.log(jnp.sum(jnp.exp(parts - peak_val[None]), axis=0))


def shifted(block, shift, width):
    reach = abs(shift) + width
    pad = jnp.full((reach,) + block.shape[1:], EMPTY_LOG, block.dtype)
    padded_block = jnp.concatenate([pad, block, pad], axis=0)
    return lax.slice_in_dim(padded_block, reach + shift, reach + shift + width, axis=0)


def received(block, axis, distance):
    index = lax.axis_index(axis)
    count = lax.axis_size(axis)
    got = passed_along(block, axis, distance)
    valid = (index - distance >= 0) & (index - distance < count)
    return jnp.where(valid, got, EMPTY_LOG)


def lse_stack(parts):
    parts = jnp.stack(parts)
    peak_val = jnp.max(parts, axis=0)
    return peak_val + jnp.log(jnp.sum(jnp.exp(parts - peak_val[None]), axis=0))


def spread_rows(block, axis, owned):
    index = lax.axis_index(axis)
    count = lax.axis_size(axis)
    edge = lax.ppermute(block, axis, [(0, 2), (count - 1, count - 3)])
    edge = jnp.where(
        index == 2, shifted(edge, 2 * owned, 5 * owned), shifted(edge, -2 * owned, 5 * owned)
    )
    edge = jnp.where((index == 2) | (index == count - 3), edge, EMPTY_LOG)
    first = lse_stack(
        [
            shifted(block, -owned, 7 * owned),
            shifted(received(block, axis, 1), 0, 7 * owned),
            shifted(received(block, axis, -1), -2 * owned, 7 * owned),
        ]
    )
    return lse_stack(
        [
            shifted(first, owned, 5 * owned),
            shifted(received(first, axis, 3), 4 * owned, 5 * owned),
            shifted(received(first, axis, -3), -2 * owned, 5 * owned),
            edge,
        ]
    )


def gather_rows(row, axis):
    index = lax.axis_index(axis)
    count = lax.axis_size(axis)
    block = row
    step = 1
    while step < count:
        route = [(i, i ^ step) for i in range(count)]
        other = lax.ppermute(block, axis, route)
        upper = (index // step) % 2 == 1
        block = jnp.where(
            upper, jnp.concatenate([other, block], axis=0), jnp.concatenate([block, other], axis=0)
        )
        step *= 2
    return block


def body(src_points, tgt_points, src_log_mass, tgt_log_mass, near_pairs, target_slot):
    owned = tgt_points.shape[0]
    group_size = src_points.shape[0]
    gy_count = lax.axis_size("gy")
    gx_index = lax.axis_index("gx")
    gy_index = lax.axis_index("gy")
    source_local = jnp.clip(near_pairs[:, 0] - gx_index * group_size, 0, group_size - 1)
    matches = (
        near_pairs[:, 1][:, None] == jnp.arange(target_slot.shape[0], dtype=jnp.int32)[None, :]
    )
    slot_ids = jnp.sum(jnp.where(matches, target_slot[None, :], 0), axis=1)
    window_ids = (slot_ids // owned // gy_count - gx_index + 1) * owned + slot_ids % owned
    window_ids = jnp.clip(window_ids, 0, 3 * owned - 1)
    span_ids = jnp.clip(source_local - (gy_index - 2) * owned, 0, 5 * owned - 1)
    span_mask = span_ids[None, :] == jnp.arange(5 * owned, dtype=jnp.int32)[:, None]
    window_mask = window_ids[None, :] == jnp.arange(3 * owned, dtype=jnp.int32)[:, None]
    pair_src_sq = squares(src_points[source_local])
    window_pts, window_sq = fetch_points(tgt_points)
    pair_tgt_sq = window_sq[window_ids]
    window_mass = fetch_potential(tgt_log_mass)
    mass_pad = jnp.zeros((2 * owned,) + src_log_mass.shape[1:], src_log_mass.dtype)
    span_mass = lax.dynamic_slice_in_dim(
        jnp.concatenate([mass_pad, src_log_mass, mass_pad], axis=0), gy_index * owned, 5 * owned, 0
    )
    g_window = jnp.zeros((3 * owned, src_points.shape[1]), jnp.float32)
    for _ in range(ITERS):
        v_row = (g_window[window_ids] - 0.5 * pair_tgt_sq) / EPSILON
        part = pair_lse(source_local, window_ids, src_points, window_pts, jnp.broadcast_to(v_row[:, None, :], (v_row.shape[0], 8, v_row.shape[1])))
        part = part[:, 0] - 0.5 * pair_src_sq / EPSILON
        rows_total = spread_rows(grouped_lse(span_mask, part), "gy", owned)
        f_span = EPSILON * span_mass - EPSILON * rows_total
        v_col = (f_span[span_ids] - 0.5 * pair_src_sq) / EPSILON
        part = pair_lse(
            window_ids, source_local, window_pts, src_points,
            jnp.broadcast_to(v_col[:, None, :], (v_col.shape[0], 8, v_col.shape[1])),
        )
        part = part[:, 0] - 0.5 * pair_tgt_sq / EPSILON
        cols_total = spread(grouped_lse(window_mask, part), "gx", 2 * owned)
        g_window = EPSILON * window_mass - EPSILON * cols_total
    f_pot = gather_rows(f_span[2 * owned : 3 * owned], "gy")
    g_local = g_window[owned : 2 * owned]
    v_row = (g_window[window_ids] - 0.5 * pair_tgt_sq) / EPSILON
    w_col = (f_span[span_ids] - 0.5 * pair_src_sq) / EPSILON
    contrib = pair_grad(
        source_local, window_ids, src_points, window_pts, v_row[:, None, :], w_col[:, :, None]
    )
    span_parts = jnp.sum(jnp.where(span_mask[:, :, None, None], contrib[None], 0.0), axis=1)
    grad = span_parts[2 * owned : 3 * owned]
    for distance in (1, 2):
        upper = passed_along(
            span_parts[(2 - distance) * owned : (3 - distance) * owned], "gy", -distance
        )
        lower = passed_along(
            span_parts[(2 + distance) * owned : (3 + distance) * owned], "gy", distance
        )
        grad = grad + upper + lower
    return (f_pot, g_local, grad)


def solution(mesh):
    in_specs = (
        P("gx", None, None),
        P(("gx", "gy"), None, None),
        P("gx", None),
        P(("gx", "gy"), None),
        P(("gx", "gy"), None),
        P(),
    )
    out_specs = (P("gx", None), P(("gx", "gy"), None), P(("gx", "gy"), None, None))

    return jax.shard_map(body, mesh=mesh, in_specs=in_specs, out_specs=out_specs, check_vma=False)
```

```python
import jax
import jax.numpy as jnp
from jax import lax
from jax.sharding import PartitionSpec as P
from jax.experimental import pallas as pl
from jax.experimental.pallas import tpu as pltpu

ITERS = 3


EMPTY_LOG = -1e30


def padded(block, sides, width):
    for axis, dim in sides:
        count = lax.axis_size(axis)
        forward = [(i, i + 1) for i in range(count - 1)]
        backward = [(target, source) for source, target in forward]
        low = lax.ppermute(
            lax.slice_in_dim(block, block.shape[dim] - width, None, axis=dim), axis, forward
        )
        high = lax.ppermute(lax.slice_in_dim(block, 0, width, axis=dim), axis, backward)
        block = jnp.concatenate([low, block, high], axis=dim)
    return block


def passed_along(block, axis, distance):
    devices = range(lax.axis_size(axis))
    route = [(i - distance, i) for i in devices if i - distance in devices]
    return lax.ppermute(block, axis, route)


def pick(table, position):
    return lax.dynamic_index_in_dim(table, position, 0, keepdims=False)


def squares(points):
    return jnp.sum(jnp.square(points.astype(jnp.float32)), axis=-1)


def fetch_points(tgt_points):
    window_pts = padded(tgt_points, (("gx", 0),), tgt_points.shape[0])
    return (window_pts, squares(window_pts))


EPSILON = 0.03
INV_EPS = 1.0 / EPSILON
CHUNK = 1024
KERNEL_PARAMS = pltpu.CompilerParams()


def _lse_kernel(a_ids, b_ids, a_ref, b_ref, v_ref, o_ref):
    tile = lax.dot_general(
        b_ref[0], a_ref[0], (((1,), (1,)), ((), ())), preferred_element_type=jnp.float32
    )
    scores = tile * INV_EPS + jnp.transpose(v_ref[0])[:, :1]
    peak = jnp.max(scores, axis=0, keepdims=True)
    total = jnp.sum(jnp.exp(scores - peak), axis=0, keepdims=True)
    o_ref[0] = peak + jnp.log(total)


def pair_lse(a_ids, b_ids, a_pts, b_pts, v_rows, interpret=False):
    pairs = a_ids.shape[0]
    rows = a_pts.shape[1]
    coords = a_pts.shape[2]
    cols = b_pts.shape[1]
    spec = pltpu.PrefetchScalarGridSpec(
        num_scalar_prefetch=2,
        grid=(pairs, rows // CHUNK),
        in_specs=[
            pl.BlockSpec((1, CHUNK, coords), lambda p, c, ai, bi: (ai[p], c, 0)),
            pl.BlockSpec((1, cols, coords), lambda p, c, ai, bi: (bi[p], 0, 0)),
            pl.BlockSpec((1, 8, cols), lambda p, c, ai, bi: (p, 0, 0)),
        ],
        out_specs=pl.BlockSpec((1, 1, CHUNK), lambda p, c, ai, bi: (p, 0, c)),
    )
    return pl.pallas_call(
        _lse_kernel,
        grid_spec=spec,
        out_shape=jax.ShapeDtypeStruct((pairs, 1, rows), jnp.float32),
        interpret=interpret,
        compiler_params=KERNEL_PARAMS,
    )(a_ids, b_ids, a_pts, b_pts, v_rows)


def _grad_kernel(a_ids, b_ids, a_ref, b_ref, v_ref, w_ref, o_ref):
    src = a_ref[0]
    tgt = b_ref[0]
    tile = lax.dot_general(src, tgt, (((1,), (1,)), ((), ())), preferred_element_type=jnp.float32)
    weights = jnp.exp(tile * INV_EPS + v_ref[0] + w_ref[0])
    mass = jnp.sum(weights, axis=1, keepdims=True)
    moved = jnp.dot(weights.astype(jnp.bfloat16), tgt, preferred_element_type=jnp.float32)
    o_ref[0] = mass * src.astype(jnp.float32) - moved


def pair_grad(a_ids, b_ids, a_pts, b_pts, v_row, w_col, interpret=False):
    pairs = a_ids.shape[0]
    rows = a_pts.shape[1]
    coords = a_pts.shape[2]
    cols = b_pts.shape[1]
    spec = pltpu.PrefetchScalarGridSpec(
        num_scalar_prefetch=2,
        grid=(pairs, rows // CHUNK),
        in_specs=[
            pl.BlockSpec((1, CHUNK, coords), lambda p, c, ai, bi: (ai[p], c, 0)),
            pl.BlockSpec((1, cols, coords), lambda p, c, ai, bi: (bi[p], 0, 0)),
            pl.BlockSpec((1, 1, cols), lambda p, c, ai, bi: (p, 0, 0)),
            pl.BlockSpec((1, CHUNK, 1), lambda p, c, ai, bi: (p, c, 0)),
        ],
        out_specs=pl.BlockSpec((1, CHUNK, coords), lambda p, c, ai, bi: (p, c, 0)),
    )
    return pl.pallas_call(
        _grad_kernel,
        grid_spec=spec,
        out_shape=jax.ShapeDtypeStruct((pairs, rows, coords), jnp.float32),
        interpret=interpret,
        compiler_params=KERNEL_PARAMS,
    )(a_ids, b_ids, a_pts, b_pts, v_row, w_col)


def grouped_lse(mask, values):
    masked = jnp.where(mask[:, :, None], values[None], EMPTY_LOG)
    peak_val = jnp.max(masked, axis=1)
    return peak_val + jnp.log(jnp.sum(jnp.exp(masked - peak_val[:, None]), axis=1))


def spread(block, axis, reach, extra):
    width = block.shape[0]
    owned = extra.shape[0]
    index = lax.axis_index(axis)
    count = lax.axis_size(axis)
    sent = jnp.concatenate([block, extra], axis=0)
    parts = [block]
    pad = jnp.full((reach,) + block.shape[1:], EMPTY_LOG, block.dtype)
    far = [reach, -reach] if count == 2 * reach else []
    extras = {}
    for distance in range(-reach, reach + 1):
        if distance == 0 or distance in far:
            continue
        got_all = passed_along(sent, axis, distance)
        valid = (index - distance >= 0) & (index - distance < count)
        got = jnp.where(valid, got_all[:width], EMPTY_LOG)
        extras[distance] = jnp.where(valid, got_all[width:], 0.0)
        got = jnp.concatenate([pad, got, pad], axis=0)
        parts.append(lax.slice_in_dim(got, reach + distance, reach + distance + width, axis=0))
    if far:
        got = lax.ppermute(block, axis, [(i, (i + reach) % count) for i in range(count)])
        got = jnp.concatenate([pad, got, pad], axis=0)
        upper = lax.slice_in_dim(got, 2 * reach, 2 * reach + width, axis=0)
        lower = lax.slice_in_dim(got, 0, width, axis=0)
        parts.append(jnp.where(index >= reach, upper, lower))
    parts = jnp.stack(parts)
    peak_val = jnp.max(parts, axis=0)
    total = peak_val + jnp.log(jnp.sum(jnp.exp(parts - peak_val[None]), axis=0))
    return total, jnp.concatenate([extras[owned], extra, extras[-owned]], axis=0)


def shifted(block, shift, width):
    reach = abs(shift) + width
    pad = jnp.full((reach,) + block.shape[1:], EMPTY_LOG, block.dtype)
    padded_block = jnp.concatenate([pad, block, pad], axis=0)
    return lax.slice_in_dim(padded_block, reach + shift, reach + shift + width, axis=0)


def received(block, axis, distance):
    index = lax.axis_index(axis)
    count = lax.axis_size(axis)
    got = passed_along(block, axis, distance)
    valid = (index - distance >= 0) & (index - distance < count)
    return jnp.where(valid, got, EMPTY_LOG)


def lse_stack(parts):
    parts = jnp.stack(parts)
    peak_val = jnp.max(parts, axis=0)
    return peak_val + jnp.log(jnp.sum(jnp.exp(parts - peak_val[None]), axis=0))


def spread_rows(block, axis, owned):
    index = lax.axis_index(axis)
    count = lax.axis_size(axis)
    edge = lax.ppermute(block, axis, [(0, 2), (count - 1, count - 3)])
    edge = jnp.where(
        index == 2, shifted(edge, 2 * owned, 5 * owned), shifted(edge, -2 * owned, 5 * owned)
    )
    edge = jnp.where((index == 2) | (index == count - 3), edge, EMPTY_LOG)
    first = lse_stack(
        [
            shifted(block, -owned, 7 * owned),
            shifted(received(block, axis, 1), 0, 7 * owned),
            shifted(received(block, axis, -1), -2 * owned, 7 * owned),
        ]
    )
    return lse_stack(
        [
            shifted(first, owned, 5 * owned),
            shifted(received(first, axis, 3), 4 * owned, 5 * owned),
            shifted(received(first, axis, -3), -2 * owned, 5 * owned),
            edge,
        ]
    )


def gather_rows(row, axis):
    index = lax.axis_index(axis)
    count = lax.axis_size(axis)
    block = row
    step = 1
    while step < count:
        route = [(i, i ^ step) for i in range(count)]
        other = lax.ppermute(block, axis, route)
        upper = (index // step) % 2 == 1
        block = jnp.where(
            upper, jnp.concatenate([other, block], axis=0), jnp.concatenate([block, other], axis=0)
        )
        step *= 2
    return block


def body(src_points, tgt_points, src_log_mass, tgt_log_mass, near_pairs, target_slot):
    owned = tgt_points.shape[0]
    group_size = src_points.shape[0]
    gy_count = lax.axis_size("gy")
    gx_index = lax.axis_index("gx")
    gy_index = lax.axis_index("gy")
    source_local = jnp.clip(near_pairs[:, 0] - gx_index * group_size, 0, group_size - 1)
    matches = (
        near_pairs[:, 1][:, None] == jnp.arange(target_slot.shape[0], dtype=jnp.int32)[None, :]
    )
    slot_ids = jnp.sum(jnp.where(matches, target_slot[None, :], 0), axis=1)
    window_ids = (slot_ids // owned // gy_count - gx_index + 1) * owned + slot_ids % owned
    window_ids = jnp.clip(window_ids, 0, 3 * owned - 1)
    span_ids = jnp.clip(source_local - (gy_index - 2) * owned, 0, 5 * owned - 1)
    span_mask = span_ids[None, :] == jnp.arange(5 * owned, dtype=jnp.int32)[:, None]
    window_mask = window_ids[None, :] == jnp.arange(3 * owned, dtype=jnp.int32)[:, None]
    pair_src_sq = jnp.stack([squares(pick(src_points, source_local[p])) for p in range(source_local.shape[0])])
    window_pts, window_sq = fetch_points(tgt_points)
    pair_tgt_sq = window_sq[window_ids]
    mass_pad = jnp.zeros((2 * owned,) + src_log_mass.shape[1:], src_log_mass.dtype)
    span_mass = lax.dynamic_slice_in_dim(
        jnp.concatenate([mass_pad, src_log_mass, mass_pad], axis=0), gy_index * owned, 5 * owned, 0
    )
    g_window = jnp.zeros((3 * owned, src_points.shape[1]), jnp.float32)
    for _ in range(ITERS):
        v_row = (g_window[window_ids] - 0.5 * pair_tgt_sq) / EPSILON
        part = pair_lse(source_local, window_ids, src_points, window_pts, jnp.broadcast_to(v_row[:, None, :], (v_row.shape[0], 8, v_row.shape[1])))
        part = part[:, 0] - 0.5 * pair_src_sq / EPSILON
        rows_total = spread_rows(grouped_lse(span_mask, part), "gy", owned)
        f_span = EPSILON * span_mass - EPSILON * rows_total
        v_col = (f_span[span_ids] - 0.5 * pair_src_sq) / EPSILON
        part = pair_lse(
            window_ids, source_local, window_pts, src_points,
            jnp.broadcast_to(v_col[:, None, :], (v_col.shape[0], 8, v_col.shape[1])),
        )
        part = part[:, 0] - 0.5 * pair_tgt_sq / EPSILON
        cols_total, window_mass = spread(
            grouped_lse(window_mask, part), "gx", 2 * owned, tgt_log_mass
        )
        g_window = EPSILON * window_mass - EPSILON * cols_total
    f_pot = gather_rows(f_span[2 * owned : 3 * owned], "gy")
    g_local = g_window[owned : 2 * owned]
    v_row = (g_window[window_ids] - 0.5 * pair_tgt_sq) / EPSILON
    w_col = (f_span[span_ids] - 0.5 * pair_src_sq) / EPSILON
    contrib = pair_grad(
        source_local, window_ids, src_points, window_pts, v_row[:, None, :], w_col[:, :, None]
    )
    span_parts = jnp.sum(jnp.where(span_mask[:, :, None, None], contrib[None], 0.0), axis=1)
    grad = span_parts[2 * owned : 3 * owned]
    for distance in (1, 2):
        upper = passed_along(
            span_parts[(2 - distance) * owned : (3 - distance) * owned], "gy", -distance
        )
        lower = passed_along(
            span_parts[(2 + distance) * owned : (3 + distance) * owned], "gy", distance
        )
        grad = grad + upper + lower
    return (f_pot, g_local, grad)


def solution(mesh):
    in_specs = (
        P("gx", None, None),
        P(("gx", "gy"), None, None),
        P("gx", None),
        P(("gx", "gy"), None),
        P(("gx", "gy"), None),
        P(),
    )
    out_specs = (P("gx", None), P(("gx", "gy"), None), P(("gx", "gy"), None, None))

    return jax.shard_map(body, mesh=mesh, in_specs=in_specs, out_specs=out_specs, check_vma=False)
```

```python
import jax
import jax.numpy as jnp
from jax import lax
from jax.sharding import PartitionSpec as P
from jax.experimental import pallas as pl
from jax.experimental.pallas import tpu as pltpu

ITERS = 3


EMPTY_LOG = -1e30


def padded(block, sides, width):
    for axis, dim in sides:
        count = lax.axis_size(axis)
        forward = [(i, i + 1) for i in range(count - 1)]
        backward = [(target, source) for source, target in forward]
        low = lax.ppermute(
            lax.slice_in_dim(block, block.shape[dim] - width, None, axis=dim), axis, forward
        )
        high = lax.ppermute(lax.slice_in_dim(block, 0, width, axis=dim), axis, backward)
        block = jnp.concatenate([low, block, high], axis=dim)
    return block


def passed_along(block, axis, distance):
    devices = range(lax.axis_size(axis))
    route = [(i - distance, i) for i in devices if i - distance in devices]
    return lax.ppermute(block, axis, route)


def squares(points):
    return jnp.sum(jnp.square(points.astype(jnp.float32)), axis=-1)


def fetch_points(tgt_points):
    window_pts = padded(tgt_points, (("gx", 0),), tgt_points.shape[0])
    return (window_pts, squares(window_pts))


EPSILON = 0.03
INV_EPS = 1.0 / EPSILON
CHUNK = 1024
KERNEL_PARAMS = pltpu.CompilerParams()


def _lse_kernel(a_ids, b_ids, a_ref, b_ref, v_ref, o_ref):
    tile = lax.dot_general(
        b_ref[0], a_ref[0], (((1,), (1,)), ((), ())), preferred_element_type=jnp.float32
    )
    scores = tile * INV_EPS + jnp.transpose(v_ref[0])[:, :1]
    peak = jnp.max(scores, axis=0, keepdims=True)
    total = jnp.sum(jnp.exp(scores - peak), axis=0, keepdims=True)
    o_ref[0] = peak + jnp.log(total)


def pair_lse(a_ids, b_ids, a_pts, b_pts, v_rows, interpret=False):
    pairs = a_ids.shape[0]
    rows = a_pts.shape[1]
    coords = a_pts.shape[2]
    cols = b_pts.shape[1]
    spec = pltpu.PrefetchScalarGridSpec(
        num_scalar_prefetch=2,
        grid=(pairs, rows // CHUNK),
        in_specs=[
            pl.BlockSpec((1, CHUNK, coords), lambda p, c, ai, bi: (ai[p], c, 0)),
            pl.BlockSpec((1, cols, coords), lambda p, c, ai, bi: (bi[p], 0, 0)),
            pl.BlockSpec((1, 8, cols), lambda p, c, ai, bi: (p, 0, 0)),
        ],
        out_specs=pl.BlockSpec((1, 1, CHUNK), lambda p, c, ai, bi: (p, 0, c)),
    )
    return pl.pallas_call(
        _lse_kernel,
        grid_spec=spec,
        out_shape=jax.ShapeDtypeStruct((pairs, 1, rows), jnp.float32),
        interpret=interpret,
        compiler_params=KERNEL_PARAMS,
    )(a_ids, b_ids, a_pts, b_pts, v_rows)


def _grad_kernel(a_ids, b_ids, a_ref, b_ref, v_ref, w_ref, o_ref):
    src = a_ref[0]
    tgt = b_ref[0]
    tile = lax.dot_general(src, tgt, (((1,), (1,)), ((), ())), preferred_element_type=jnp.float32)
    weights = jnp.exp(tile * INV_EPS + v_ref[0] + w_ref[0])
    mass = jnp.sum(weights, axis=1, keepdims=True)
    moved = jnp.dot(weights.astype(jnp.bfloat16), tgt, preferred_element_type=jnp.float32)
    o_ref[0] = mass * src.astype(jnp.float32) - moved


def pair_grad(a_ids, b_ids, a_pts, b_pts, v_row, w_col, interpret=False):
    pairs = a_ids.shape[0]
    rows = a_pts.shape[1]
    coords = a_pts.shape[2]
    cols = b_pts.shape[1]
    spec = pltpu.PrefetchScalarGridSpec(
        num_scalar_prefetch=2,
        grid=(pairs, rows // CHUNK),
        in_specs=[
            pl.BlockSpec((1, CHUNK, coords), lambda p, c, ai, bi: (ai[p], c, 0)),
            pl.BlockSpec((1, cols, coords), lambda p, c, ai, bi: (bi[p], 0, 0)),
            pl.BlockSpec((1, 1, cols), lambda p, c, ai, bi: (p, 0, 0)),
            pl.BlockSpec((1, CHUNK, 1), lambda p, c, ai, bi: (p, c, 0)),
        ],
        out_specs=pl.BlockSpec((1, CHUNK, coords), lambda p, c, ai, bi: (p, c, 0)),
    )
    return pl.pallas_call(
        _grad_kernel,
        grid_spec=spec,
        out_shape=jax.ShapeDtypeStruct((pairs, rows, coords), jnp.float32),
        interpret=interpret,
        compiler_params=KERNEL_PARAMS,
    )(a_ids, b_ids, a_pts, b_pts, v_row, w_col)


def grouped_lse(mask, values):
    masked = jnp.where(mask[:, :, None], values[None], EMPTY_LOG)
    peak_val = jnp.max(masked, axis=1)
    return peak_val + jnp.log(jnp.sum(jnp.exp(masked - peak_val[:, None]), axis=1))


def spread(block, axis, reach, extra):
    width = block.shape[0]
    owned = extra.shape[0]
    index = lax.axis_index(axis)
    count = lax.axis_size(axis)
    sent = jnp.concatenate([block, extra], axis=0)
    parts = [block]
    pad = jnp.full((reach,) + block.shape[1:], EMPTY_LOG, block.dtype)
    far = [reach, -reach] if count == 2 * reach else []
    extras = {}
    for distance in range(-reach, reach + 1):
        if distance == 0 or distance in far:
            continue
        got_all = passed_along(sent, axis, distance)
        valid = (index - distance >= 0) & (index - distance < count)
        got = jnp.where(valid, got_all[:width], EMPTY_LOG)
        extras[distance] = jnp.where(valid, got_all[width:], 0.0)
        got = jnp.concatenate([pad, got, pad], axis=0)
        parts.append(lax.slice_in_dim(got, reach + distance, reach + distance + width, axis=0))
    if far:
        got = lax.ppermute(block, axis, [(i, (i + reach) % count) for i in range(count)])
        got = jnp.concatenate([pad, got, pad], axis=0)
        upper = lax.slice_in_dim(got, 2 * reach, 2 * reach + width, axis=0)
        lower = lax.slice_in_dim(got, 0, width, axis=0)
        parts.append(jnp.where(index >= reach, upper, lower))
    parts = jnp.stack(parts)
    peak_val = jnp.max(parts, axis=0)
    total = peak_val + jnp.log(jnp.sum(jnp.exp(parts - peak_val[None]), axis=0))
    return total, jnp.concatenate([extras[owned], extra, extras[-owned]], axis=0)


def shifted(block, shift, width):
    reach = abs(shift) + width
    pad = jnp.full((reach,) + block.shape[1:], EMPTY_LOG, block.dtype)
    padded_block = jnp.concatenate([pad, block, pad], axis=0)
    return lax.slice_in_dim(padded_block, reach + shift, reach + shift + width, axis=0)


def received(block, axis, distance):
    index = lax.axis_index(axis)
    count = lax.axis_size(axis)
    got = passed_along(block, axis, distance)
    valid = (index - distance >= 0) & (index - distance < count)
    return jnp.where(valid, got, EMPTY_LOG)


def lse_stack(parts):
    parts = jnp.stack(parts)
    peak_val = jnp.max(parts, axis=0)
    return peak_val + jnp.log(jnp.sum(jnp.exp(parts - peak_val[None]), axis=0))


def spread_rows(block, axis, owned):
    index = lax.axis_index(axis)
    count = lax.axis_size(axis)
    edge = lax.ppermute(block, axis, [(0, 2), (count - 1, count - 3)])
    edge = jnp.where(
        index == 2, shifted(edge, 2 * owned, 5 * owned), shifted(edge, -2 * owned, 5 * owned)
    )
    edge = jnp.where((index == 2) | (index == count - 3), edge, EMPTY_LOG)
    first = lse_stack(
        [
            shifted(block, -owned, 7 * owned),
            shifted(received(block, axis, 1), 0, 7 * owned),
            shifted(received(block, axis, -1), -2 * owned, 7 * owned),
        ]
    )
    return lse_stack(
        [
            shifted(first, owned, 5 * owned),
            shifted(received(first, axis, 3), 4 * owned, 5 * owned),
            shifted(received(first, axis, -3), -2 * owned, 5 * owned),
            edge,
        ]
    )


def gather_rows(row, axis):
    index = lax.axis_index(axis)
    count = lax.axis_size(axis)
    block = row
    order = [[i] for i in range(count)]
    step = count // 2
    while step >= 1:
        route = [(i, i ^ step) for i in range(count)]
        other = lax.ppermute(block, axis, route)
        upper = (index // step) % 2 == 1
        block = jnp.where(
            upper, jnp.concatenate([other, block], axis=0), jnp.concatenate([block, other], axis=0)
        )
        order = [
            order[i ^ step] + order[i] if (i // step) % 2 == 1 else order[i] + order[i ^ step]
            for i in range(count)
        ]
        step //= 2
    rows = row.shape[0]
    position = {device: place for place, device in enumerate(order[0])}
    take = [position[device] * rows + r for device in range(count) for r in range(rows)]
    return jnp.take(block, jnp.array(take, dtype=jnp.int32), axis=0)


def body(src_points, tgt_points, src_log_mass, tgt_log_mass, near_pairs, target_slot):
    owned = tgt_points.shape[0]
    group_size = src_points.shape[0]
    gy_count = lax.axis_size("gy")
    gx_index = lax.axis_index("gx")
    gy_index = lax.axis_index("gy")
    source_local = jnp.clip(near_pairs[:, 0] - gx_index * group_size, 0, group_size - 1)
    matches = (
        near_pairs[:, 1][:, None] == jnp.arange(target_slot.shape[0], dtype=jnp.int32)[None, :]
    )
    slot_ids = jnp.sum(jnp.where(matches, target_slot[None, :], 0), axis=1)
    window_ids = (slot_ids // owned // gy_count - gx_index + 1) * owned + slot_ids % owned
    window_ids = jnp.clip(window_ids, 0, 3 * owned - 1)
    span_ids = jnp.clip(source_local - (gy_index - 2) * owned, 0, 5 * owned - 1)
    span_mask = span_ids[None, :] == jnp.arange(5 * owned, dtype=jnp.int32)[:, None]
    window_mask = window_ids[None, :] == jnp.arange(3 * owned, dtype=jnp.int32)[:, None]
    pair_src_sq = squares(src_points[source_local])
    window_pts, window_sq = fetch_points(tgt_points)
    pair_tgt_sq = window_sq[window_ids]
    mass_pad = jnp.zeros((2 * owned,) + src_log_mass.shape[1:], src_log_mass.dtype)
    span_mass = lax.dynamic_slice_in_dim(
        jnp.concatenate([mass_pad, src_log_mass, mass_pad], axis=0), gy_index * owned, 5 * owned, 0
    )
    g_window = jnp.zeros((3 * owned, src_points.shape[1]), jnp.float32)
    for _ in range(ITERS):
        v_row = (g_window[window_ids] - 0.5 * pair_tgt_sq) / EPSILON
        part = pair_lse(source_local, window_ids, src_points, window_pts, jnp.broadcast_to(v_row[:, None, :], (v_row.shape[0], 8, v_row.shape[1])))
        part = part[:, 0] - 0.5 * pair_src_sq / EPSILON
        rows_total = spread_rows(grouped_lse(span_mask, part), "gy", owned)
        f_span = EPSILON * span_mass - EPSILON * rows_total
        v_col = (f_span[span_ids] - 0.5 * pair_src_sq) / EPSILON
        part = pair_lse(
            window_ids, source_local, window_pts, src_points,
            jnp.broadcast_to(v_col[:, None, :], (v_col.shape[0], 8, v_col.shape[1])),
        )
        part = part[:, 0] - 0.5 * pair_tgt_sq / EPSILON
        cols_total, window_mass = spread(
            grouped_lse(window_mask, part), "gx", 2 * owned, tgt_log_mass
        )
        g_window = EPSILON * window_mass - EPSILON * cols_total
    f_pot = gather_rows(f_span[2 * owned : 3 * owned], "gy")
    g_local = g_window[owned : 2 * owned]
    v_row = (g_window[window_ids] - 0.5 * pair_tgt_sq) / EPSILON
    w_col = (f_span[span_ids] - 0.5 * pair_src_sq) / EPSILON
    contrib = pair_grad(
        source_local, window_ids, src_points, window_pts, v_row[:, None, :], w_col[:, :, None]
    )
    span_parts = jnp.sum(jnp.where(span_mask[:, :, None, None], contrib[None], 0.0), axis=1)
    grad = span_parts[2 * owned : 3 * owned]
    for distance in (1, 2):
        upper = passed_along(
            span_parts[(2 - distance) * owned : (3 - distance) * owned], "gy", -distance
        )
        lower = passed_along(
            span_parts[(2 + distance) * owned : (3 + distance) * owned], "gy", distance
        )
        grad = grad + upper + lower
    return (f_pot, g_local, grad)


def solution(mesh):
    in_specs = (
        P("gx", None, None),
        P(("gx", "gy"), None, None),
        P("gx", None),
        P(("gx", "gy"), None),
        P(("gx", "gy"), None),
        P(),
    )
    out_specs = (P("gx", None), P(("gx", "gy"), None), P(("gx", "gy"), None, None))

    return jax.shard_map(body, mesh=mesh, in_specs=in_specs, out_specs=out_specs, check_vma=False)
```

```python
import jax
import jax.numpy as jnp
from jax import lax
from jax.sharding import PartitionSpec as P
from jax.experimental import pallas as pl
from jax.experimental.pallas import tpu as pltpu

ITERS = 3


EMPTY_LOG = -1e30


def padded(block, sides, width):
    for axis, dim in sides:
        count = lax.axis_size(axis)
        forward = [(i, i + 1) for i in range(count - 1)]
        backward = [(target, source) for source, target in forward]
        low = lax.ppermute(
            lax.slice_in_dim(block, block.shape[dim] - width, None, axis=dim), axis, forward
        )
        high = lax.ppermute(lax.slice_in_dim(block, 0, width, axis=dim), axis, backward)
        block = jnp.concatenate([low, block, high], axis=dim)
    return block


def passed_along(block, axis, distance):
    devices = range(lax.axis_size(axis))
    route = [(i - distance, i) for i in devices if i - distance in devices]
    return lax.ppermute(block, axis, route)


def squares(points):
    return jnp.sum(jnp.square(points.astype(jnp.float32)), axis=-1)


def fetch_points(tgt_points):
    window_pts = padded(tgt_points, (("gx", 0),), tgt_points.shape[0])
    return (window_pts, squares(window_pts))


EPSILON = 0.03
INV_EPS = 1.0 / EPSILON
CHUNK = 1024
GRAD_CHUNK = 512
KERNEL_PARAMS = pltpu.CompilerParams()


def _lse_kernel(a_ids, b_ids, a_ref, b_ref, v_ref, o_ref):
    tile = lax.dot_general(
        b_ref[0], a_ref[0], (((1,), (1,)), ((), ())), preferred_element_type=jnp.float32
    )
    scores = tile * INV_EPS + jnp.transpose(v_ref[0])[:, :1]
    peak = jnp.max(scores, axis=0, keepdims=True)
    total = jnp.sum(jnp.exp(scores - peak), axis=0, keepdims=True)
    o_ref[0] = peak + jnp.log(total)


def pair_lse(a_ids, b_ids, a_pts, b_pts, v_rows, interpret=False):
    pairs = a_ids.shape[0]
    rows = a_pts.shape[1]
    coords = a_pts.shape[2]
    cols = b_pts.shape[1]
    spec = pltpu.PrefetchScalarGridSpec(
        num_scalar_prefetch=2,
        grid=(pairs, rows // CHUNK),
        in_specs=[
            pl.BlockSpec((1, CHUNK, coords), lambda p, c, ai, bi: (ai[p], c, 0)),
            pl.BlockSpec((1, cols, coords), lambda p, c, ai, bi: (bi[p], 0, 0)),
            pl.BlockSpec((1, 8, cols), lambda p, c, ai, bi: (p, 0, 0)),
        ],
        out_specs=pl.BlockSpec((1, 1, CHUNK), lambda p, c, ai, bi: (p, 0, c)),
    )
    return pl.pallas_call(
        _lse_kernel,
        grid_spec=spec,
        out_shape=jax.ShapeDtypeStruct((pairs, 1, rows), jnp.float32),
        interpret=interpret,
        compiler_params=KERNEL_PARAMS,
    )(a_ids, b_ids, a_pts, b_pts, v_rows)


def _grad_kernel(a_ids, b_ids, a_ref, b_ref, v_ref, w_ref, o_ref):
    src = a_ref[0]
    tgt = b_ref[0]
    tile = lax.dot_general(src, tgt, (((1,), (1,)), ((), ())), preferred_element_type=jnp.float32)
    weights = jnp.exp(tile * INV_EPS + v_ref[0] + w_ref[0])
    mass = jnp.sum(weights, axis=1, keepdims=True)
    moved = jnp.dot(weights.astype(jnp.bfloat16), tgt, preferred_element_type=jnp.float32)
    o_ref[0] = mass * src.astype(jnp.float32) - moved


def pair_grad(a_ids, b_ids, a_pts, b_pts, v_row, w_col, interpret=False):
    pairs = a_ids.shape[0]
    rows = a_pts.shape[1]
    coords = a_pts.shape[2]
    cols = b_pts.shape[1]
    spec = pltpu.PrefetchScalarGridSpec(
        num_scalar_prefetch=2,
        grid=(pairs, rows // GRAD_CHUNK),
        in_specs=[
            pl.BlockSpec((1, GRAD_CHUNK, coords), lambda p, c, ai, bi: (ai[p], c, 0)),
            pl.BlockSpec((1, cols, coords), lambda p, c, ai, bi: (bi[p], 0, 0)),
            pl.BlockSpec((1, 1, cols), lambda p, c, ai, bi: (p, 0, 0)),
            pl.BlockSpec((1, GRAD_CHUNK, 1), lambda p, c, ai, bi: (p, c, 0)),
        ],
        out_specs=pl.BlockSpec((1, GRAD_CHUNK, coords), lambda p, c, ai, bi: (p, c, 0)),
    )
    return pl.pallas_call(
        _grad_kernel,
        grid_spec=spec,
        out_shape=jax.ShapeDtypeStruct((pairs, rows, coords), jnp.float32),
        interpret=interpret,
        compiler_params=KERNEL_PARAMS,
    )(a_ids, b_ids, a_pts, b_pts, v_row, w_col)


def grouped_lse(mask, values):
    masked = jnp.where(mask[:, :, None], values[None], EMPTY_LOG)
    peak_val = jnp.max(masked, axis=1)
    return peak_val + jnp.log(jnp.sum(jnp.exp(masked - peak_val[:, None]), axis=1))


def spread(block, axis, reach, extra):
    width = block.shape[0]
    owned = extra.shape[0]
    index = lax.axis_index(axis)
    count = lax.axis_size(axis)
    sent = jnp.concatenate([block, extra], axis=0)
    parts = [block]
    pad = jnp.full((reach,) + block.shape[1:], EMPTY_LOG, block.dtype)
    far = [reach, -reach] if count == 2 * reach else []
    extras = {}
    for distance in range(-reach, reach + 1):
        if distance == 0 or distance in far:
            continue
        got_all = passed_along(sent, axis, distance)
        valid = (index - distance >= 0) & (index - distance < count)
        got = jnp.where(valid, got_all[:width], EMPTY_LOG)
        extras[distance] = jnp.where(valid, got_all[width:], 0.0)
        got = jnp.concatenate([pad, got, pad], axis=0)
        parts.append(lax.slice_in_dim(got, reach + distance, reach + distance + width, axis=0))
    if far:
        got = lax.ppermute(block, axis, [(i, (i + reach) % count) for i in range(count)])
        got = jnp.concatenate([pad, got, pad], axis=0)
        upper = lax.slice_in_dim(got, 2 * reach, 2 * reach + width, axis=0)
        lower = lax.slice_in_dim(got, 0, width, axis=0)
        parts.append(jnp.where(index >= reach, upper, lower))
    parts = jnp.stack(parts)
    peak_val = jnp.max(parts, axis=0)
    total = peak_val + jnp.log(jnp.sum(jnp.exp(parts - peak_val[None]), axis=0))
    return total, jnp.concatenate([extras[owned], extra, extras[-owned]], axis=0)


def shifted(block, shift, width):
    reach = abs(shift) + width
    pad = jnp.full((reach,) + block.shape[1:], EMPTY_LOG, block.dtype)
    padded_block = jnp.concatenate([pad, block, pad], axis=0)
    return lax.slice_in_dim(padded_block, reach + shift, reach + shift + width, axis=0)


def received(block, axis, distance):
    index = lax.axis_index(axis)
    count = lax.axis_size(axis)
    got = passed_along(block, axis, distance)
    valid = (index - distance >= 0) & (index - distance < count)
    return jnp.where(valid, got, EMPTY_LOG)


def lse_stack(parts):
    parts = jnp.stack(parts)
    peak_val = jnp.max(parts, axis=0)
    return peak_val + jnp.log(jnp.sum(jnp.exp(parts - peak_val[None]), axis=0))


def spread_rows(block, axis, owned):
    index = lax.axis_index(axis)
    count = lax.axis_size(axis)
    edge = lax.ppermute(block, axis, [(0, 2), (count - 1, count - 3)])
    edge = jnp.where(
        index == 2, shifted(edge, 2 * owned, 5 * owned), shifted(edge, -2 * owned, 5 * owned)
    )
    edge = jnp.where((index == 2) | (index == count - 3), edge, EMPTY_LOG)
    first = lse_stack(
        [
            shifted(block, -owned, 7 * owned),
            shifted(received(block, axis, 1), 0, 7 * owned),
            shifted(received(block, axis, -1), -2 * owned, 7 * owned),
        ]
    )
    return lse_stack(
        [
            shifted(first, owned, 5 * owned),
            shifted(received(first, axis, 3), 4 * owned, 5 * owned),
            shifted(received(first, axis, -3), -2 * owned, 5 * owned),
            edge,
        ]
    )


def gather_rows(row, axis):
    index = lax.axis_index(axis)
    count = lax.axis_size(axis)
    block = row
    step = 1
    while step < count:
        route = [(i, i ^ step) for i in range(count)]
        other = lax.ppermute(block, axis, route)
        upper = (index // step) % 2 == 1
        block = jnp.where(
            upper, jnp.concatenate([other, block], axis=0), jnp.concatenate([block, other], axis=0)
        )
        step *= 2
    return block


def body(src_points, tgt_points, src_log_mass, tgt_log_mass, near_pairs, target_slot):
    owned = tgt_points.shape[0]
    group_size = src_points.shape[0]
    gy_count = lax.axis_size("gy")
    gx_index = lax.axis_index("gx")
    gy_index = lax.axis_index("gy")
    source_local = jnp.clip(near_pairs[:, 0] - gx_index * group_size, 0, group_size - 1)
    matches = (
        near_pairs[:, 1][:, None] == jnp.arange(target_slot.shape[0], dtype=jnp.int32)[None, :]
    )
    slot_ids = jnp.sum(jnp.where(matches, target_slot[None, :], 0), axis=1)
    window_ids = (slot_ids // owned // gy_count - gx_index + 1) * owned + slot_ids % owned
    window_ids = jnp.clip(window_ids, 0, 3 * owned - 1)
    span_ids = jnp.clip(source_local - (gy_index - 2) * owned, 0, 5 * owned - 1)
    span_mask = span_ids[None, :] == jnp.arange(5 * owned, dtype=jnp.int32)[:, None]
    window_mask = window_ids[None, :] == jnp.arange(3 * owned, dtype=jnp.int32)[:, None]
    pair_src_sq = squares(src_points[source_local])
    window_pts, window_sq = fetch_points(tgt_points)
    pair_tgt_sq = window_sq[window_ids]
    mass_pad = jnp.zeros((2 * owned,) + src_log_mass.shape[1:], src_log_mass.dtype)
    span_mass = lax.dynamic_slice_in_dim(
        jnp.concatenate([mass_pad, src_log_mass, mass_pad], axis=0), gy_index * owned, 5 * owned, 0
    )
    g_window = jnp.zeros((3 * owned, src_points.shape[1]), jnp.float32)
    for _ in range(ITERS):
        v_row = (g_window[window_ids] - 0.5 * pair_tgt_sq) / EPSILON
        part = pair_lse(source_local, window_ids, src_points, window_pts, jnp.broadcast_to(v_row[:, None, :], (v_row.shape[0], 8, v_row.shape[1])))
        part = part[:, 0] - 0.5 * pair_src_sq / EPSILON
        rows_total = spread_rows(grouped_lse(span_mask, part), "gy", owned)
        f_span = EPSILON * span_mass - EPSILON * rows_total
        v_col = (f_span[span_ids] - 0.5 * pair_src_sq) / EPSILON
        part = pair_lse(
            window_ids, source_local, window_pts, src_points,
            jnp.broadcast_to(v_col[:, None, :], (v_col.shape[0], 8, v_col.shape[1])),
        )
        part = part[:, 0] - 0.5 * pair_tgt_sq / EPSILON
        cols_total, window_mass = spread(
            grouped_lse(window_mask, part), "gx", 2 * owned, tgt_log_mass
        )
        g_window = EPSILON * window_mass - EPSILON * cols_total
    f_pot = gather_rows(f_span[2 * owned : 3 * owned], "gy")
    g_local = g_window[owned : 2 * owned]
    v_row = (g_window[window_ids] - 0.5 * pair_tgt_sq) / EPSILON
    w_col = (f_span[span_ids] - 0.5 * pair_src_sq) / EPSILON
    contrib = pair_grad(
        source_local, window_ids, src_points, window_pts, v_row[:, None, :], w_col[:, :, None]
    )
    span_parts = jnp.sum(jnp.where(span_mask[:, :, None, None], contrib[None], 0.0), axis=1)
    grad = span_parts[2 * owned : 3 * owned]
    for distance in (1, 2):
        upper = passed_along(
            span_parts[(2 - distance) * owned : (3 - distance) * owned], "gy", -distance
        )
        lower = passed_along(
            span_parts[(2 + distance) * owned : (3 + distance) * owned], "gy", distance
        )
        grad = grad + upper + lower
    return (f_pot, g_local, grad)


def solution(mesh):
    in_specs = (
        P("gx", None, None),
        P(("gx", "gy"), None, None),
        P("gx", None),
        P(("gx", "gy"), None),
        P(("gx", "gy"), None),
        P(),
    )
    out_specs = (P("gx", None), P(("gx", "gy"), None), P(("gx", "gy"), None, None))

    return jax.shard_map(body, mesh=mesh, in_specs=in_specs, out_specs=out_specs, check_vma=False)
```

```python
import jax
import jax.numpy as jnp
from jax import lax
from jax.sharding import PartitionSpec as P
from jax.experimental import pallas as pl
from jax.experimental.pallas import tpu as pltpu

ITERS = 3


EMPTY_LOG = -1e30


def padded(block, sides, width):
    for axis, dim in sides:
        count = lax.axis_size(axis)
        forward = [(i, i + 1) for i in range(count - 1)]
        backward = [(target, source) for source, target in forward]
        low = lax.ppermute(
            lax.slice_in_dim(block, block.shape[dim] - width, None, axis=dim), axis, forward
        )
        high = lax.ppermute(lax.slice_in_dim(block, 0, width, axis=dim), axis, backward)
        block = jnp.concatenate([low, block, high], axis=dim)
    return block


def passed_along(block, axis, distance):
    devices = range(lax.axis_size(axis))
    route = [(i - distance, i) for i in devices if i - distance in devices]
    return lax.ppermute(block, axis, route)


def squares(points):
    return jnp.sum(jnp.square(points.astype(jnp.float32)), axis=-1)


def fetch_points(tgt_points):
    window_pts = padded(tgt_points, (("gx", 0),), tgt_points.shape[0])
    return (window_pts, squares(window_pts))


EPSILON = 0.03
INV_EPS = 1.0 / EPSILON
CHUNK = 1024
LSE_PARAMS = pltpu.CompilerParams(allow_input_fusion=[False, False, False, False, True])
KERNEL_PARAMS = pltpu.CompilerParams()


def _lse_kernel(a_ids, b_ids, a_ref, b_ref, v_ref, o_ref):
    tile = lax.dot_general(
        b_ref[0], a_ref[0], (((1,), (1,)), ((), ())), preferred_element_type=jnp.float32
    )
    scores = tile * INV_EPS + jnp.transpose(v_ref[0])[:, :1]
    peak = jnp.max(scores, axis=0, keepdims=True)
    total = jnp.sum(jnp.exp(scores - peak), axis=0, keepdims=True)
    o_ref[0] = peak + jnp.log(total)


def pair_lse(a_ids, b_ids, a_pts, b_pts, v_rows, interpret=False):
    pairs = a_ids.shape[0]
    rows = a_pts.shape[1]
    coords = a_pts.shape[2]
    cols = b_pts.shape[1]
    spec = pltpu.PrefetchScalarGridSpec(
        num_scalar_prefetch=2,
        grid=(pairs, rows // CHUNK),
        in_specs=[
            pl.BlockSpec((1, CHUNK, coords), lambda p, c, ai, bi: (ai[p], c, 0)),
            pl.BlockSpec((1, cols, coords), lambda p, c, ai, bi: (bi[p], 0, 0)),
            pl.BlockSpec((1, 8, cols), lambda p, c, ai, bi: (p, 0, 0)),
        ],
        out_specs=pl.BlockSpec((1, 1, CHUNK), lambda p, c, ai, bi: (p, 0, c)),
    )
    return pl.pallas_call(
        _lse_kernel,
        grid_spec=spec,
        out_shape=jax.ShapeDtypeStruct((pairs, 1, rows), jnp.float32),
        interpret=interpret,
        compiler_params=LSE_PARAMS,
    )(a_ids, b_ids, a_pts, b_pts, v_rows)


def _grad_kernel(a_ids, b_ids, a_ref, b_ref, v_ref, w_ref, o_ref):
    src = a_ref[0]
    tgt = b_ref[0]
    tile = lax.dot_general(src, tgt, (((1,), (1,)), ((), ())), preferred_element_type=jnp.float32)
    weights = jnp.exp(tile * INV_EPS + v_ref[0] + w_ref[0])
    mass = jnp.sum(weights, axis=1, keepdims=True)
    moved = jnp.dot(weights.astype(jnp.bfloat16), tgt, preferred_element_type=jnp.float32)
    o_ref[0] = mass * src.astype(jnp.float32) - moved


def pair_grad(a_ids, b_ids, a_pts, b_pts, v_row, w_col, interpret=False):
    pairs = a_ids.shape[0]
    rows = a_pts.shape[1]
    coords = a_pts.shape[2]
    cols = b_pts.shape[1]
    spec = pltpu.PrefetchScalarGridSpec(
        num_scalar_prefetch=2,
        grid=(pairs, rows // CHUNK),
        in_specs=[
            pl.BlockSpec((1, CHUNK, coords), lambda p, c, ai, bi: (ai[p], c, 0)),
            pl.BlockSpec((1, cols, coords), lambda p, c, ai, bi: (bi[p], 0, 0)),
            pl.BlockSpec((1, 1, cols), lambda p, c, ai, bi: (p, 0, 0)),
            pl.BlockSpec((1, CHUNK, 1), lambda p, c, ai, bi: (p, c, 0)),
        ],
        out_specs=pl.BlockSpec((1, CHUNK, coords), lambda p, c, ai, bi: (p, c, 0)),
    )
    return pl.pallas_call(
        _grad_kernel,
        grid_spec=spec,
        out_shape=jax.ShapeDtypeStruct((pairs, rows, coords), jnp.float32),
        interpret=interpret,
        compiler_params=KERNEL_PARAMS,
    )(a_ids, b_ids, a_pts, b_pts, v_row, w_col)


def grouped_lse(mask, values):
    masked = jnp.where(mask[:, :, None], values[None], EMPTY_LOG)
    peak_val = jnp.max(masked, axis=1)
    return peak_val + jnp.log(jnp.sum(jnp.exp(masked - peak_val[:, None]), axis=1))


def spread(block, axis, reach, extra):
    width = block.shape[0]
    owned = extra.shape[0]
    index = lax.axis_index(axis)
    count = lax.axis_size(axis)
    sent = jnp.concatenate([block, extra], axis=0)
    parts = [block]
    pad = jnp.full((reach,) + block.shape[1:], EMPTY_LOG, block.dtype)
    far = [reach, -reach] if count == 2 * reach else []
    extras = {}
    for distance in range(-reach, reach + 1):
        if distance == 0 or distance in far:
            continue
        got_all = passed_along(sent, axis, distance)
        valid = (index - distance >= 0) & (index - distance < count)
        got = jnp.where(valid, got_all[:width], EMPTY_LOG)
        extras[distance] = jnp.where(valid, got_all[width:], 0.0)
        got = jnp.concatenate([pad, got, pad], axis=0)
        parts.append(lax.slice_in_dim(got, reach + distance, reach + distance + width, axis=0))
    if far:
        got = lax.ppermute(block, axis, [(i, (i + reach) % count) for i in range(count)])
        got = jnp.concatenate([pad, got, pad], axis=0)
        upper = lax.slice_in_dim(got, 2 * reach, 2 * reach + width, axis=0)
        lower = lax.slice_in_dim(got, 0, width, axis=0)
        parts.append(jnp.where(index >= reach, upper, lower))
    parts = jnp.stack(parts)
    peak_val = jnp.max(parts, axis=0)
    total = peak_val + jnp.log(jnp.sum(jnp.exp(parts - peak_val[None]), axis=0))
    return total, jnp.concatenate([extras[owned], extra, extras[-owned]], axis=0)


def shifted(block, shift, width):
    reach = abs(shift) + width
    pad = jnp.full((reach,) + block.shape[1:], EMPTY_LOG, block.dtype)
    padded_block = jnp.concatenate([pad, block, pad], axis=0)
    return lax.slice_in_dim(padded_block, reach + shift, reach + shift + width, axis=0)


def received(block, axis, distance):
    index = lax.axis_index(axis)
    count = lax.axis_size(axis)
    got = passed_along(block, axis, distance)
    valid = (index - distance >= 0) & (index - distance < count)
    return jnp.where(valid, got, EMPTY_LOG)


def lse_stack(parts):
    parts = jnp.stack(parts)
    peak_val = jnp.max(parts, axis=0)
    return peak_val + jnp.log(jnp.sum(jnp.exp(parts - peak_val[None]), axis=0))


def spread_rows(block, axis, owned):
    index = lax.axis_index(axis)
    count = lax.axis_size(axis)
    edge = lax.ppermute(block, axis, [(0, 2), (count - 1, count - 3)])
    edge = jnp.where(
        index == 2, shifted(edge, 2 * owned, 5 * owned), shifted(edge, -2 * owned, 5 * owned)
    )
    edge = jnp.where((index == 2) | (index == count - 3), edge, EMPTY_LOG)
    first = lse_stack(
        [
            shifted(block, -owned, 7 * owned),
            shifted(received(block, axis, 1), 0, 7 * owned),
            shifted(received(block, axis, -1), -2 * owned, 7 * owned),
        ]
    )
    return lse_stack(
        [
            shifted(first, owned, 5 * owned),
            shifted(received(first, axis, 3), 4 * owned, 5 * owned),
            shifted(received(first, axis, -3), -2 * owned, 5 * owned),
            edge,
        ]
    )


def gather_rows(row, axis):
    index = lax.axis_index(axis)
    count = lax.axis_size(axis)
    block = row
    step = 1
    while step < count:
        route = [(i, i ^ step) for i in range(count)]
        other = lax.ppermute(block, axis, route)
        upper = (index // step) % 2 == 1
        block = jnp.where(
            upper, jnp.concatenate([other, block], axis=0), jnp.concatenate([block, other], axis=0)
        )
        step *= 2
    return block


def body(src_points, tgt_points, src_log_mass, tgt_log_mass, near_pairs, target_slot):
    owned = tgt_points.shape[0]
    group_size = src_points.shape[0]
    gy_count = lax.axis_size("gy")
    gx_index = lax.axis_index("gx")
    gy_index = lax.axis_index("gy")
    source_local = jnp.clip(near_pairs[:, 0] - gx_index * group_size, 0, group_size - 1)
    matches = (
        near_pairs[:, 1][:, None] == jnp.arange(target_slot.shape[0], dtype=jnp.int32)[None, :]
    )
    slot_ids = jnp.sum(jnp.where(matches, target_slot[None, :], 0), axis=1)
    window_ids = (slot_ids // owned // gy_count - gx_index + 1) * owned + slot_ids % owned
    window_ids = jnp.clip(window_ids, 0, 3 * owned - 1)
    span_ids = jnp.clip(source_local - (gy_index - 2) * owned, 0, 5 * owned - 1)
    span_mask = span_ids[None, :] == jnp.arange(5 * owned, dtype=jnp.int32)[:, None]
    window_mask = window_ids[None, :] == jnp.arange(3 * owned, dtype=jnp.int32)[:, None]
    pair_src_sq = squares(src_points[source_local])
    window_pts, window_sq = fetch_points(tgt_points)
    pair_tgt_sq = window_sq[window_ids]
    mass_pad = jnp.zeros((2 * owned,) + src_log_mass.shape[1:], src_log_mass.dtype)
    span_mass = lax.dynamic_slice_in_dim(
        jnp.concatenate([mass_pad, src_log_mass, mass_pad], axis=0), gy_index * owned, 5 * owned, 0
    )
    g_window = jnp.zeros((3 * owned, src_points.shape[1]), jnp.float32)
    for _ in range(ITERS):
        v_row = (g_window[window_ids] - 0.5 * pair_tgt_sq) / EPSILON
        part = pair_lse(source_local, window_ids, src_points, window_pts, jnp.broadcast_to(v_row[:, None, :], (v_row.shape[0], 8, v_row.shape[1])))
        part = part[:, 0] - 0.5 * pair_src_sq / EPSILON
        rows_total = spread_rows(grouped_lse(span_mask, part), "gy", owned)
        f_span = EPSILON * span_mass - EPSILON * rows_total
        v_col = (f_span[span_ids] - 0.5 * pair_src_sq) / EPSILON
        part = pair_lse(
            window_ids, source_local, window_pts, src_points,
            jnp.broadcast_to(v_col[:, None, :], (v_col.shape[0], 8, v_col.shape[1])),
        )
        part = part[:, 0] - 0.5 * pair_tgt_sq / EPSILON
        cols_total, window_mass = spread(
            grouped_lse(window_mask, part), "gx", 2 * owned, tgt_log_mass
        )
        g_window = EPSILON * window_mass - EPSILON * cols_total
    f_pot = gather_rows(f_span[2 * owned : 3 * owned], "gy")
    g_local = g_window[owned : 2 * owned]
    v_row = (g_window[window_ids] - 0.5 * pair_tgt_sq) / EPSILON
    w_col = (f_span[span_ids] - 0.5 * pair_src_sq) / EPSILON
    contrib = pair_grad(
        source_local, window_ids, src_points, window_pts, v_row[:, None, :], w_col[:, :, None]
    )
    span_parts = jnp.sum(jnp.where(span_mask[:, :, None, None], contrib[None], 0.0), axis=1)
    grad = span_parts[2 * owned : 3 * owned]
    for distance in (1, 2):
        upper = passed_along(
            span_parts[(2 - distance) * owned : (3 - distance) * owned], "gy", -distance
        )
        lower = passed_along(
            span_parts[(2 + distance) * owned : (3 + distance) * owned], "gy", distance
        )
        grad = grad + upper + lower
    return (f_pot, g_local, grad)


def solution(mesh):
    in_specs = (
        P("gx", None, None),
        P(("gx", "gy"), None, None),
        P("gx", None),
        P(("gx", "gy"), None),
        P(("gx", "gy"), None),
        P(),
    )
    out_specs = (P("gx", None), P(("gx", "gy"), None), P(("gx", "gy"), None, None))

    return jax.shard_map(body, mesh=mesh, in_specs=in_specs, out_specs=out_specs, check_vma=False)
```
